512 devices in a mesh: space: 64 (over z_hi, y, core), member: 8 (over z_lo, x).
Axes of the slice: x: 4, y: 8, z: 8 (z_hi: 4, z_lo: 2; z = z_hi * 2 + z_lo), core: 2. Of those that a mesh axis runs over, the one named last changes fastest.
Arguments:
- pressure: float32 [32, 10, 131072], P('member', None, 'space'), may hold values from -6 to 6
- heat: float32 [32, 10, 131072], P('member', None, 'space'), may hold values from -6 to 6
- log_cond: float32 [10, 131072], P(None, 'space'), may hold values from -1 to 1
- log_therm: float32 [10, 131072], P(None, 'space'), may hold values from -1 to 1
- frozen: float32 [10, 131072], P(None, 'space'), may hold values from 0 to 1
- frozen_flag: int32 [10, 131072], P(None, 'space'), may hold values 0 or 1
- recharge: float32 [32, 131072], P('member', 'space'), may hold values from -6 to 6
- face_cols: int32 [4, 16384], P(None, 'space'), may hold values from 0 to 2047
- face_weight: float32 [4, 16384], P(None, 'space'), may hold values from 0.05 to 0.3
- cot_pressure: float32 [32, 10, 131072], P('member', None, 'space'), may hold values from -6 to 6
- cot_heat: float32 [32, 10, 131072], P('member', None, 'space'), may hold values from -6 to 6
Outputs:
- new_pressure: float32 [32, 10, 131072], P('member', None, 'space')
- new_heat: float32 [32, 10, 131072], P('member', None, 'space')
- adj_pressure: float32 [32, 10, 131072], P('member', None, 'space')
- adj_heat: float32 [32, 10, 131072], P('member', None, 'space')
- param_grads: float32 [2, 10, 131072], P(None, None, ('space', 'member'))
The draws below stay inside these ranges and needn't reach their ends.
All inputs are finite; a program needn't handle non-finite values. No bound on the sum of `frozen_flag` on one device may be relied on, other than what follows from the above.
Results may differ from the reference program's by a relative error of at most 0.00007.
Values sent between devices are 32-bit elements; how exact they have to be, the bound alone decides.
No kernel may reach another device: no remote copies, remote signals or barrier semaphores. Data moves between devices by JAX's collectives and lax.ppermute only.
A program may use at most 64 MiB of HBM per device.

```python
import math
import jax
import jax.numpy as jnp

COL_DEV = 2048
LAYERS = 10
ROUNDS = 4
FACE = 256
MEMBERS = 32
COLUMNS = 131072
N_SPACE = 64


def touch_ends(values, key, least, largest):
    longest = values.shape.index(max(values.shape))
    spots = []
    for shift in (0, 1):
        where = [jax.random.randint(jax.random.fold_in(key, axis), (), 0, length) for axis, length in enumerate(values.shape)]
        where[longest] = (where[longest] + shift) % values.shape[longest]
        spots.append(tuple(where))
    return values.at[spots[0]].set(least).at[spots[1]].set(largest)


def levels(stream_key, shape, shards, least, top_value):
    factor_of, own = 1.0, jax.random.fold_in(stream_key, 6)
    for position, parts in shards:
        draws = jnp.exp(jax.random.uniform(jax.random.fold_in(own, position), (parts,), jnp.float32, least / len(shards), top_value / len(shards)))
        factor_of = factor_of * jnp.repeat(draws, shape[position] // parts).reshape([-1 if axis == position else 1 for axis in range(len(shape))])
    return factor_of


def normal_values(own_key, dims, width, most, cuts=(), kind=jnp.bfloat16):
    level = levels(own_key, dims, cuts, -0.22, 0.18) if cuts else 1.0
    result = jax.random.normal(own_key, dims, jnp.float32) * width * level
    return jnp.minimum(jnp.maximum(result, -most), most).astype(kind)


def setup_inputs(seed: int = 0) -> dict:
    streams_of = jax.random.split(jax.random.key(seed), 12)
    return {
        "pressure": normal_values(streams_of[0], (MEMBERS, LAYERS, COLUMNS), 1.0, 6.0, ((0, 8), (2, 64)), jnp.float32),
        "heat": normal_values(streams_of[1], (MEMBERS, LAYERS, COLUMNS), 1.0, 6.0, ((0, 8), (2, 64)), jnp.float32),
        "log_cond": jnp.clip(jax.random.uniform(streams_of[2], (LAYERS, COLUMNS), jnp.float32, -1.0, 1.0) * levels(streams_of[2], (LAYERS, COLUMNS), ((1, 64),), -0.4, 0.0), -1.0, 1.0),
        "log_therm": jnp.clip(jax.random.uniform(streams_of[3], (LAYERS, COLUMNS), jnp.float32, -1.0, 1.0) * levels(streams_of[3], (LAYERS, COLUMNS), ((1, 64),), -0.4, 0.0), -1.0, 1.0),
        "frozen": jnp.clip(1.0 * jax.random.uniform(streams_of[4], (LAYERS, COLUMNS), jnp.float32) ** levels(streams_of[4], (LAYERS, COLUMNS), ((1, 64),), -0.2, 0.2), 0.0, 1.0),
        "frozen_flag": touch_ends((jax.random.randint(streams_of[5], (LAYERS, COLUMNS), 0, 2) < 1).astype(jnp.int32), jax.random.fold_in(streams_of[5], 1), 0, 1),
        "recharge": normal_values(streams_of[6], (MEMBERS, COLUMNS), 1.0, 6.0, ((0, 8), (1, 64)), jnp.float32),
        "face_cols": touch_ends(jax.random.randint(streams_of[7], (ROUNDS, FACE * N_SPACE), 0, COL_DEV), jax.random.fold_in(streams_of[7], 1), 0, COL_DEV - 1).astype(jnp.int32),
        "face_weight": jnp.clip(jnp.exp(math.log(0.3) - 1.7917595 * jax.random.uniform(streams_of[8], (ROUNDS, FACE * N_SPACE), jnp.float32) ** levels(streams_of[8], (ROUNDS, FACE * N_SPACE), ((1, 64),), -0.2, 0.2)), 0.05, 0.3),
        "cot_pressure": normal_values(streams_of[9], (MEMBERS, LAYERS, COLUMNS), 1.0, 6.0, ((0, 8), (2, 64)), jnp.float32),
        "cot_heat": normal_values(streams_of[10], (MEMBERS, LAYERS, COLUMNS), 1.0, 6.0, ((0, 8), (2, 64)), jnp.float32),
    }


def spread(grad_iface):
    return jnp.pad(grad_iface, ((0, 0), (0, 1), (0, 0))) - jnp.pad(grad_iface, ((0, 0), (1, 0), (0, 0)))

def reference(pressure, heat, log_cond, log_therm, frozen, frozen_flag, recharge, face_cols, face_weight, cot_pressure, cot_heat):
    tiles = jnp.arange(N_SPACE, dtype=jnp.int32)
    blocked = frozen * frozen_flag.astype(jnp.float32)

    def advance(p_old, t_old, log_k, log_t):
        cond = jnp.exp(log_k - 3.0 * blocked)
        therm = jnp.exp(log_t) * (1.0 + blocked)
        flow = 0.5 * (cond[:-1] + cond[1:]) * (p_old[:, 1:] - p_old[:, :-1])
        conduct = 0.5 * (therm[:-1] + therm[1:]) * (t_old[:, 1:] - t_old[:, :-1])
        carried = flow * 0.5 * (t_old[:, :-1] + t_old[:, 1:])
        p_rate = spread(flow)
        p_rate = p_rate.at[:, 0].add(recharge)
        t_rate = spread(conduct) + 0.5 * spread(carried)
        for index in range(ROUNDS):
            local_cols = face_cols[index].reshape(N_SPACE, FACE)
            global_cols = (tiles[:, None] * COL_DEV + local_cols).reshape(-1)
            partner = jnp.bitwise_xor(tiles, jnp.int32(1 << index))
            partner_cols = global_cols.reshape(N_SPACE, FACE)[partner].reshape(-1)
            weight = face_weight[index]
            p_own = p_old[:, :, global_cols]
            t_own = t_old[:, :, global_cols]
            p_far = p_old[:, :, partner_cols]
            t_far = t_old[:, :, partner_cols]
            p_rate = p_rate.at[:, :, global_cols].add(weight * cond[:, global_cols] * (p_far - p_own))
            t_rate = t_rate.at[:, :, global_cols].add(weight * therm[:, global_cols] * (t_far - t_own))
        return (p_old + 0.1 * p_rate, t_old + 0.1 * t_rate)
    (new_pressure, new_heat), pullback = jax.vjp(advance, pressure, heat, log_cond, log_therm)
    adj_pressure, adj_heat, grad_k, grad_t = pullback((cot_pressure, cot_heat))
    return (new_pressure, new_heat, adj_pressure, adj_heat, jnp.stack([grad_k, grad_t]))
```

```python
import jax
import jax.numpy as jnp
from jax import lax
from jax.sharding import PartitionSpec as P


def from_partner(value, axis, mask):
    pairs = [(source, source ^ mask) for source in range(lax.axis_size(axis))]
    return lax.ppermute(value, axis, pairs)


def spread(grad_iface):
    return jnp.pad(grad_iface, ((0, 0), (0, 1), (0, 0))) - jnp.pad(
        grad_iface, ((0, 0), (1, 0), (0, 0))
    )


def pad_sum(grad_iface, axis):
    pads = [(0, 0)] * grad_iface.ndim
    low, high = list(pads), list(pads)
    low[axis], high[axis] = (0, 1), (1, 0)
    return jnp.pad(grad_iface, low) + jnp.pad(grad_iface, high)


def split3(x):
    hi = lax.reduce_precision(x, exponent_bits=8, mantissa_bits=7)
    rest = x - hi
    mid = lax.reduce_precision(rest, exponent_bits=8, mantissa_bits=7)
    lo = rest - mid
    return jnp.concatenate(
        [hi.astype(jnp.bfloat16), mid.astype(jnp.bfloat16), lo.astype(jnp.bfloat16)]
    )


def exact_select(rows, select, contract):
    n = rows.shape[0]
    parts = lax.dot_general(
        split3(rows),
        select,
        (((1,), (contract,)), ((), ())),
        preferred_element_type=jnp.float32,
    )
    return (parts[:n] + parts[n : 2 * n]) + parts[2 * n :]


def reduce_scatter(value, axis):
    size = lax.axis_size(axis)
    index = lax.axis_index(axis)
    width = value.shape[-1] // size
    cur = value.reshape(value.shape[:-1] + (size, width))
    dist = size // 2
    while dist >= 1:
        half = cur.shape[-2] // 2
        lower, upper = cur[..., :half, :], cur[..., half:, :]
        bit = (index // dist) % 2 == 1
        keep = jnp.where(bit, upper, lower)
        send = jnp.where(bit, lower, upper)
        cur = keep + from_partner(send, axis, dist)
        dist //= 2
    return cur.reshape(value.shape[:-1] + (width,))


def body(
    pressure,
    heat,
    log_cond,
    log_therm,
    frozen,
    frozen_flag,
    recharge,
    face_cols,
    face_weight,
    cot_pressure,
    cot_heat,
):
    members, layers, width = pressure.shape
    rounds, face = face_cols.shape
    blocked = frozen * frozen_flag.astype(jnp.float32)
    cond = jnp.exp(log_cond - 3.0 * blocked)
    therm = jnp.exp(log_therm) * (1.0 + blocked)
    g_p = 0.1 * cot_pressure
    g_t = 0.1 * cot_heat

    cols = face_cols.reshape(rounds * face)
    select = (cols[:, None] == jnp.arange(width, dtype=jnp.int32)[None, :]).astype(
        jnp.bfloat16
    )

    n_field = members * layers
    rows = jnp.concatenate(
        [
            jnp.stack([pressure, heat, g_p, g_t]).reshape(4 * n_field, width),
            jnp.stack([cond, therm]).reshape(2 * layers, width),
        ]
    )
    picked = exact_select(rows, select, 1)
    fields_f = picked[: 4 * n_field].reshape(4, members, layers, rounds, face)
    coefs_f = picked[4 * n_field :].reshape(2, 1, layers, rounds, face)
    wc = face_weight * coefs_f
    own = fields_f[:2]
    g_own = fields_f[2:] * wc
    sending = jnp.concatenate([own, g_own])

    far = []
    for index in range(rounds):
        far.append(from_partner(sending[..., index, :], "space", 1 << index))
    far = jnp.stack(far, axis=-2)

    diff = far[:2] - own
    update = wc * diff
    adj_lat = far[2:] - g_own
    param_lat = face_weight * jnp.sum(fields_f[2:] * diff, axis=1)

    kf = 0.5 * (cond[:-1] + cond[1:])
    kt = 0.5 * (therm[:-1] + therm[1:])
    d_p = pressure[:, 1:] - pressure[:, :-1]
    d_t = heat[:, 1:] - heat[:, :-1]
    flow = kf * d_p
    conduct = kt * d_t
    t_mean = 0.5 * (heat[:, :-1] + heat[:, 1:])
    carried = flow * t_mean
    da = g_p[:, :-1] - g_p[:, 1:]
    db = g_t[:, :-1] - g_t[:, 1:]
    g_carried = 0.5 * db
    g_flow = da + g_carried * t_mean
    g_kf = jnp.sum(g_flow * d_p, axis=0)
    g_kt = jnp.sum(db * d_t, axis=0)
    vert_grads = jnp.stack([0.5 * pad_sum(g_kf, 0), 0.5 * pad_sum(g_kt, 0)])

    lat_grads = exact_select(
        param_lat.reshape(2 * layers, rounds * face), select, 0
    ).reshape(2, layers, width)
    grads = (vert_grads + lat_grads) * jnp.stack([cond, therm])
    owned = reduce_scatter(grads, "member")

    lat = exact_select(
        jnp.concatenate([update, adj_lat]).reshape(4 * n_field, rounds * face),
        select,
        0,
    ).reshape(4, members, layers, width)

    p_rate = spread(flow)
    p_rate = p_rate.at[:, 0].add(recharge)
    t_rate = spread(conduct) + 0.5 * spread(carried)
    new_pressure = pressure + 0.1 * (p_rate + lat[0])
    new_heat = heat + 0.1 * (t_rate + lat[1])
    adj_pressure = cot_pressure - spread(g_flow * kf[None]) + lat[2]
    adj_heat = (
        cot_heat
        - spread(db * kt[None])
        + 0.5 * pad_sum(g_carried * flow, 1)
        + lat[3]
    )
    return (new_pressure, new_heat, adj_pressure, adj_heat, owned)


def solution(mesh):
    placed = (
        P("member", None, "space"),
        P("member", None, "space"),
        P(None, "space"),
        P(None, "space"),
        P(None, "space"),
        P(None, "space"),
        P("member", "space"),
        P(None, "space"),
        P(None, "space"),
        P("member", None, "space"),
        P("member", None, "space"),
    )
    return jax.shard_map(
        body,
        mesh=mesh,
        in_specs=placed,
        out_specs=(
            P("member", None, "space"),
            P("member", None, "space"),
            P("member", None, "space"),
            P("member", None, "space"),
            P(None, None, ("space", "member")),
        ),
        check_vma=False,
    )
```

```python
import jax
import jax.numpy as jnp
from jax import lax
from jax.sharding import PartitionSpec as P


def from_partner(value, axis, mask):
    pairs = [(source, source ^ mask) for source in range(lax.axis_size(axis))]
    return lax.ppermute(value, axis, pairs)


def spread(grad_iface):
    return jnp.pad(grad_iface, ((0, 0), (0, 1), (0, 0))) - jnp.pad(
        grad_iface, ((0, 0), (1, 0), (0, 0))
    )


def spread0(grad_iface):
    return pad_sum(grad_iface, 0, -1.0)


def pad_sum(grad_iface, axis, sign=1.0):
    pads = [(0, 0)] * grad_iface.ndim
    low, high = list(pads), list(pads)
    low[axis], high[axis] = (0, 1), (1, 0)
    if sign < 0:
        return jnp.pad(grad_iface, low) - jnp.pad(grad_iface, high)
    return jnp.pad(grad_iface, low) + jnp.pad(grad_iface, high)


def split3(x):
    hi = lax.reduce_precision(x, exponent_bits=8, mantissa_bits=7)
    rest = x - hi
    mid = lax.reduce_precision(rest, exponent_bits=8, mantissa_bits=7)
    lo = rest - mid
    return jnp.concatenate(
        [hi.astype(jnp.bfloat16), mid.astype(jnp.bfloat16), lo.astype(jnp.bfloat16)]
    )


def exact_select(rows, select, contract):
    n = rows.shape[0]
    parts = lax.dot_general(
        split3(rows),
        select,
        (((1,), (contract,)), ((), ())),
        preferred_element_type=jnp.float32,
    )
    return (parts[:n] + parts[n : 2 * n]) + parts[2 * n :]


def reduce_scatter(value, axis):
    size = lax.axis_size(axis)
    index = lax.axis_index(axis)
    width = value.shape[-1] // size
    cur = value.reshape(value.shape[:-1] + (size, width))
    dist = size // 2
    while dist >= 1:
        half = cur.shape[-2] // 2
        lower, upper = cur[..., :half, :], cur[..., half:, :]
        bit = (index // dist) % 2 == 1
        keep = jnp.where(bit, upper, lower)
        send = jnp.where(bit, lower, upper)
        cur = keep + from_partner(send, axis, dist)
        dist //= 2
    return cur.reshape(value.shape[:-1] + (width,))


def body(
    pressure,
    heat,
    log_cond,
    log_therm,
    frozen,
    frozen_flag,
    recharge,
    face_cols,
    face_weight,
    cot_pressure,
    cot_heat,
):
    members, layers, width = pressure.shape
    rounds, face = face_cols.shape
    p_old = pressure.transpose(1, 0, 2)
    t_old = heat.transpose(1, 0, 2)
    c_p = cot_pressure.transpose(1, 0, 2)
    c_t = cot_heat.transpose(1, 0, 2)
    blocked = frozen * frozen_flag.astype(jnp.float32)
    cond = jnp.exp(log_cond - 3.0 * blocked)
    therm = jnp.exp(log_therm) * (1.0 + blocked)
    g_p = 0.1 * c_p
    g_t = 0.1 * c_t

    cols = face_cols.reshape(rounds * face)
    select = (cols[:, None] == jnp.arange(width, dtype=jnp.int32)[None, :]).astype(
        jnp.bfloat16
    )

    n_field = members * layers
    rows = jnp.concatenate(
        [
            jnp.stack([p_old, t_old, g_p, g_t]).reshape(4 * n_field, width),
            jnp.stack([cond, therm]).reshape(2 * layers, width),
        ]
    )
    picked = exact_select(rows, select, 1)
    fields_f = picked[: 4 * n_field].reshape(4, layers, members, rounds, face)
    coefs_f = picked[4 * n_field :].reshape(2, layers, 1, rounds, face)
    wc = face_weight * coefs_f
    own = fields_f[:2]
    g_own = fields_f[2:] * wc
    sending = jnp.concatenate([own, g_own])

    far = []
    for index in range(rounds):
        far.append(from_partner(sending[..., index, :], "space", 1 << index))
    far = jnp.stack(far, axis=-2)

    diff = far[:2] - own
    update = wc * diff
    adj_lat = far[2:] - g_own
    param_lat = face_weight * jnp.sum(fields_f[2:] * diff, axis=2)

    kf = (0.5 * (cond[:-1] + cond[1:]))[:, None]
    kt = (0.5 * (therm[:-1] + therm[1:]))[:, None]
    d_p = p_old[1:] - p_old[:-1]
    d_t = t_old[1:] - t_old[:-1]
    flow = kf * d_p
    conduct = kt * d_t
    t_mean = 0.5 * (t_old[:-1] + t_old[1:])
    carried = flow * t_mean
    da = g_p[:-1] - g_p[1:]
    db = g_t[:-1] - g_t[1:]
    g_carried = 0.5 * db
    g_flow = da + g_carried * t_mean
    g_kf = jnp.sum(g_flow * d_p, axis=1)
    g_kt = jnp.sum(db * d_t, axis=1)
    vert_grads = jnp.stack([0.5 * pad_sum(g_kf, 0), 0.5 * pad_sum(g_kt, 0)])

    lat_grads = exact_select(
        param_lat.reshape(2 * layers, rounds * face), select, 0
    ).reshape(2, layers, width)
    grads = (vert_grads + lat_grads) * jnp.stack([cond, therm])
    owned = reduce_scatter(grads, "member")

    lat = exact_select(
        jnp.concatenate([update, adj_lat]).reshape(4 * n_field, rounds * face),
        select,
        0,
    ).reshape(4, layers, members, width)

    p_rate = spread0(flow)
    p_rate = p_rate.at[0].add(recharge)
    t_rate = spread0(conduct) + 0.5 * spread0(carried)
    new_pressure = p_old + 0.1 * (p_rate + lat[0])
    new_heat = t_old + 0.1 * (t_rate + lat[1])
    adj_pressure = c_p - spread0(g_flow * kf) + lat[2]
    adj_heat = c_t - spread0(db * kt) + 0.5 * pad_sum(g_carried * flow, 0) + lat[3]
    outs = [new_pressure, new_heat, adj_pressure, adj_heat]
    return tuple(o.transpose(1, 0, 2) for o in outs) + (owned,)


def solution(mesh):
    placed = (
        P("member", None, "space"),
        P("member", None, "space"),
        P(None, "space"),
        P(None, "space"),
        P(None, "space"),
        P(None, "space"),
        P("member", "space"),
        P(None, "space"),
        P(None, "space"),
        P("member", None, "space"),
        P("member", None, "space"),
    )
    return jax.shard_map(
        body,
        mesh=mesh,
        in_specs=placed,
        out_specs=(
            P("member", None, "space"),
            P("member", None, "space"),
            P("member", None, "space"),
            P("member", None, "space"),
            P(None, None, ("space", "member")),
        ),
        check_vma=False,
    )
```

```python
import jax
import jax.numpy as jnp
from jax import lax
from jax.sharding import PartitionSpec as P


def from_partner(value, axis, mask):
    pairs = [(source, source ^ mask) for source in range(lax.axis_size(axis))]
    return lax.ppermute(value, axis, pairs)


def spread(grad_iface):
    return jnp.pad(grad_iface, ((0, 0), (0, 1), (0, 0))) - jnp.pad(
        grad_iface, ((0, 0), (1, 0), (0, 0))
    )


def spread0(grad_iface):
    return pad_sum(grad_iface, 0, -1.0)


def pad_sum(grad_iface, axis, sign=1.0):
    pads = [(0, 0)] * grad_iface.ndim
    low, high = list(pads), list(pads)
    low[axis], high[axis] = (0, 1), (1, 0)
    if sign < 0:
        return jnp.pad(grad_iface, low) - jnp.pad(grad_iface, high)
    return jnp.pad(grad_iface, low) + jnp.pad(grad_iface, high)


def split3(x):
    hi = lax.reduce_precision(x, exponent_bits=8, mantissa_bits=7)
    rest = x - hi
    mid = lax.reduce_precision(rest, exponent_bits=8, mantissa_bits=7)
    lo = rest - mid
    return jnp.concatenate(
        [hi.astype(jnp.bfloat16), mid.astype(jnp.bfloat16), lo.astype(jnp.bfloat16)]
    )


def exact_select(rows, select, contract):
    n = rows.shape[0]
    parts = lax.dot_general(
        split3(rows),
        select,
        (((1,), (contract,)), ((), ())),
        preferred_element_type=jnp.float32,
    )
    return (parts[:n] + parts[n : 2 * n]) + parts[2 * n :]


def reduce_scatter(value, axis):
    size = lax.axis_size(axis)
    index = lax.axis_index(axis)
    width = value.shape[-1] // size
    cur = value.reshape(value.shape[:-1] + (size, width))
    dist = size // 2
    while dist >= 1:
        half = cur.shape[-2] // 2
        lower, upper = cur[..., :half, :], cur[..., half:, :]
        bit = (index // dist) % 2 == 1
        keep = jnp.where(bit, upper, lower)
        send = jnp.where(bit, lower, upper)
        cur = keep + from_partner(send, axis, dist)
        dist //= 2
    return cur.reshape(value.shape[:-1] + (width,))


def sum_scatter(value, axis):
    size = lax.axis_size(axis)
    width = value.shape[-1] // size
    parts = value.reshape(value.shape[:-1] + (size, width))
    got = lax.all_to_all(parts, axis, parts.ndim - 2, parts.ndim - 2, tiled=True)
    return jnp.sum(got, axis=-2)


def body(
    pressure,
    heat,
    log_cond,
    log_therm,
    frozen,
    frozen_flag,
    recharge,
    face_cols,
    face_weight,
    cot_pressure,
    cot_heat,
):
    members, layers, width = pressure.shape
    rounds, face = face_cols.shape
    p_old = pressure.transpose(1, 0, 2)
    t_old = heat.transpose(1, 0, 2)
    c_p = cot_pressure.transpose(1, 0, 2)
    c_t = cot_heat.transpose(1, 0, 2)
    blocked = frozen * frozen_flag.astype(jnp.float32)
    cond = jnp.exp(log_cond - 3.0 * blocked)
    therm = jnp.exp(log_therm) * (1.0 + blocked)
    g_p = 0.1 * c_p
    g_t = 0.1 * c_t

    cols = face_cols.reshape(rounds * face)
    select = (cols[:, None] == jnp.arange(width, dtype=jnp.int32)[None, :]).astype(
        jnp.bfloat16
    )

    n_field = members * layers
    rows = jnp.concatenate(
        [
            jnp.stack([p_old, t_old, g_p, g_t]).reshape(4 * n_field, width),
            jnp.stack([cond, therm]).reshape(2 * layers, width),
        ]
    )
    picked = exact_select(rows, select, 1)
    fields_f = picked[: 4 * n_field].reshape(4, layers, members, rounds, face)
    coefs_f = picked[4 * n_field :].reshape(2, layers, 1, rounds, face)
    wc = face_weight * coefs_f
    own = fields_f[:2]
    g_own = fields_f[2:] * wc
    sending = jnp.concatenate([own, g_own])

    far = []
    for index in range(rounds):
        far.append(from_partner(sending[..., index, :], "space", 1 << index))
    far = jnp.stack(far, axis=-2)

    diff = far[:2] - own
    update = wc * diff
    adj_lat = far[2:] - g_own
    param_lat = face_weight * jnp.sum(fields_f[2:] * diff, axis=2)

    kf = (0.5 * (cond[:-1] + cond[1:]))[:, None]
    kt = (0.5 * (therm[:-1] + therm[1:]))[:, None]
    d_p = p_old[1:] - p_old[:-1]
    d_t = t_old[1:] - t_old[:-1]
    flow = kf * d_p
    conduct = kt * d_t
    t_mean = 0.5 * (t_old[:-1] + t_old[1:])
    carried = flow * t_mean
    da = g_p[:-1] - g_p[1:]
    db = g_t[:-1] - g_t[1:]
    g_carried = 0.5 * db
    g_flow = da + g_carried * t_mean
    g_kf = jnp.sum(g_flow * d_p, axis=1)
    g_kt = jnp.sum(db * d_t, axis=1)
    vert_grads = jnp.stack([0.5 * pad_sum(g_kf, 0), 0.5 * pad_sum(g_kt, 0)])

    lat_grads = exact_select(
        param_lat.reshape(2 * layers, rounds * face), select, 0
    ).reshape(2, layers, width)
    grads = (vert_grads + lat_grads) * jnp.stack([cond, therm])
    owned = sum_scatter(grads, "member")

    lat = exact_select(
        jnp.concatenate([update, adj_lat]).reshape(4 * n_field, rounds * face),
        select,
        0,
    ).reshape(4, layers, members, width)

    p_rate = spread0(flow)
    p_rate = p_rate.at[0].add(recharge)
    t_rate = spread0(conduct) + 0.5 * spread0(carried)
    new_pressure = p_old + 0.1 * (p_rate + lat[0])
    new_heat = t_old + 0.1 * (t_rate + lat[1])
    adj_pressure = c_p - spread0(g_flow * kf) + lat[2]
    adj_heat = c_t - spread0(db * kt) + 0.5 * pad_sum(g_carried * flow, 0) + lat[3]
    outs = [new_pressure, new_heat, adj_pressure, adj_heat]
    return tuple(o.transpose(1, 0, 2) for o in outs) + (owned,)


def solution(mesh):
    placed = (
        P("member", None, "space"),
        P("member", None, "space"),
        P(None, "space"),
        P(None, "space"),
        P(None, "space"),
        P(None, "space"),
        P("member", "space"),
        P(None, "space"),
        P(None, "space"),
        P("member", None, "space"),
        P("member", None, "space"),
    )
    return jax.shard_map(
        body,
        mesh=mesh,
        in_specs=placed,
        out_specs=(
            P("member", None, "space"),
            P("member", None, "space"),
            P("member", None, "space"),
            P("member", None, "space"),
            P(None, None, ("space", "member")),
        ),
        check_vma=False,
    )
```

```python
import jax
import jax.numpy as jnp
from jax import lax
from jax.sharding import PartitionSpec as P


def from_partner(value, axis, mask):
    pairs = [(source, source ^ mask) for source in range(lax.axis_size(axis))]
    return lax.ppermute(value, axis, pairs)


def spread(grad_iface):
    return jnp.pad(grad_iface, ((0, 0), (0, 1), (0, 0))) - jnp.pad(
        grad_iface, ((0, 0), (1, 0), (0, 0))
    )


def spread0(grad_iface):
    return pad_sum(grad_iface, 0, -1.0)


def pad_sum(grad_iface, axis, sign=1.0):
    pads = [(0, 0)] * grad_iface.ndim
    low, high = list(pads), list(pads)
    low[axis], high[axis] = (0, 1), (1, 0)
    if sign < 0:
        return jnp.pad(grad_iface, low) - jnp.pad(grad_iface, high)
    return jnp.pad(grad_iface, low) + jnp.pad(grad_iface, high)


def split3(x):
    hi = lax.reduce_precision(x, exponent_bits=8, mantissa_bits=7)
    rest = x - hi
    mid = lax.reduce_precision(rest, exponent_bits=8, mantissa_bits=7)
    lo = rest - mid
    return jnp.concatenate(
        [hi.astype(jnp.bfloat16), mid.astype(jnp.bfloat16), lo.astype(jnp.bfloat16)]
    )


def exact_select(rows, select, contract):
    parts = lax.dot_general(
        split3(rows),
        select,
        (((1,), (contract,)), ((), ())),
        preferred_element_type=jnp.float32,
    )
    return combine3(parts)


def combine3(parts):
    n = parts.shape[0] // 3
    return (parts[:n] + parts[n : 2 * n]) + parts[2 * n :]


def reduce_scatter(value, axis):
    size = lax.axis_size(axis)
    index = lax.axis_index(axis)
    width = value.shape[-1] // size
    cur = value.reshape(value.shape[:-1] + (size, width))
    dist = size // 2
    while dist >= 1:
        half = cur.shape[-2] // 2
        lower, upper = cur[..., :half, :], cur[..., half:, :]
        bit = (index // dist) % 2 == 1
        keep = jnp.where(bit, upper, lower)
        send = jnp.where(bit, lower, upper)
        cur = keep + from_partner(send, axis, dist)
        dist //= 2
    return cur.reshape(value.shape[:-1] + (width,))


def sum_scatter(value, axis):
    size = lax.axis_size(axis)
    width = value.shape[-1] // size
    parts = value.reshape(value.shape[:-1] + (size, width))
    got = lax.all_to_all(parts, axis, parts.ndim - 2, parts.ndim - 2, tiled=True)
    return jnp.sum(got, axis=-2)


def body(
    pressure,
    heat,
    log_cond,
    log_therm,
    frozen,
    frozen_flag,
    recharge,
    face_cols,
    face_weight,
    cot_pressure,
    cot_heat,
):
    members, layers, width = pressure.shape
    rounds, face = face_cols.shape
    p_old = pressure.transpose(1, 0, 2)
    t_old = heat.transpose(1, 0, 2)
    c_p = cot_pressure.transpose(1, 0, 2)
    c_t = cot_heat.transpose(1, 0, 2)
    blocked = frozen * frozen_flag.astype(jnp.float32)
    cond = jnp.exp(log_cond - 3.0 * blocked)
    therm = jnp.exp(log_therm) * (1.0 + blocked)
    g_p = 0.1 * c_p
    g_t = 0.1 * c_t

    cols = face_cols.reshape(rounds * face)
    select = (cols[:, None] == jnp.arange(width, dtype=jnp.int32)[None, :]).astype(
        jnp.bfloat16
    )

    n_field = members * layers
    rows = jnp.concatenate(
        [
            jnp.stack([p_old, t_old, g_p, g_t]).reshape(4 * n_field, width),
            jnp.stack([cond, therm]).reshape(2 * layers, width),
        ]
    )
    row_parts = split3(rows)

    placed = None
    for index in reversed(range(rounds)):
        choose = select[index * face : (index + 1) * face]
        weight = face_weight[index]
        picked = combine3(
            lax.dot_general(
                row_parts,
                choose,
                (((1,), (1,)), ((), ())),
                preferred_element_type=jnp.float32,
            )
        )
        fields_f = picked[: 4 * n_field].reshape(4, layers, members, face)
        coefs_f = picked[4 * n_field :].reshape(2, layers, 1, face)
        wc = weight * coefs_f
        own = fields_f[:2]
        g_own = fields_f[2:] * wc
        far = from_partner(jnp.concatenate([own, g_own]), "space", 1 << index)
        diff = far[:2] - own
        param_lat = weight * jnp.sum(fields_f[2:] * diff, axis=2)
        back = jnp.concatenate(
            [
                param_lat.reshape(2 * layers, face),
                jnp.concatenate([wc * diff, far[2:] - g_own]).reshape(
                    4 * n_field, face
                ),
            ]
        )
        term = exact_select(back, choose, 0)
        placed = term if placed is None else placed + term
    lat_grads = placed[: 2 * layers].reshape(2, layers, width)
    lat = placed[2 * layers :].reshape(4, layers, members, width)

    kf = (0.5 * (cond[:-1] + cond[1:]))[:, None]
    kt = (0.5 * (therm[:-1] + therm[1:]))[:, None]
    d_p = p_old[1:] - p_old[:-1]
    d_t = t_old[1:] - t_old[:-1]
    flow = kf * d_p
    conduct = kt * d_t
    t_mean = 0.5 * (t_old[:-1] + t_old[1:])
    carried = flow * t_mean
    da = g_p[:-1] - g_p[1:]
    db = g_t[:-1] - g_t[1:]
    g_carried = 0.5 * db
    g_flow = da + g_carried * t_mean
    g_kf = jnp.sum(g_flow * d_p, axis=1)
    g_kt = jnp.sum(db * d_t, axis=1)
    vert_grads = jnp.stack([0.5 * pad_sum(g_kf, 0), 0.5 * pad_sum(g_kt, 0)])

    grads = (vert_grads + lat_grads) * jnp.stack([cond, therm])
    owned = sum_scatter(grads, "member")


    p_rate = spread0(flow)
    p_rate = p_rate.at[0].add(recharge)
    t_rate = spread0(conduct) + 0.5 * spread0(carried)
    new_pressure = p_old + 0.1 * (p_rate + lat[0])
    new_heat = t_old + 0.1 * (t_rate + lat[1])
    adj_pressure = c_p - spread0(g_flow * kf) + lat[2]
    adj_heat = c_t - spread0(db * kt) + 0.5 * pad_sum(g_carried * flow, 0) + lat[3]
    outs = [new_pressure, new_heat, adj_pressure, adj_heat]
    return tuple(o.transpose(1, 0, 2) for o in outs) + (owned,)


def solution(mesh):
    placed = (
        P("member", None, "space"),
        P("member", None, "space"),
        P(None, "space"),
        P(None, "space"),
        P(None, "space"),
        P(None, "space"),
        P("member", "space"),
        P(None, "space"),
        P(None, "space"),
        P("member", None, "space"),
        P("member", None, "space"),
    )
    return jax.shard_map(
        body,
        mesh=mesh,
        in_specs=placed,
        out_specs=(
            P("member", None, "space"),
            P("member", None, "space"),
            P("member", None, "space"),
            P("member", None, "space"),
            P(None, None, ("space", "member")),
        ),
        check_vma=False,
    )
```

```python
import jax
import jax.numpy as jnp
from jax import lax
from jax.sharding import PartitionSpec as P


def from_partner(value, axis, mask):
    pairs = [(source, source ^ mask) for source in range(lax.axis_size(axis))]
    return lax.ppermute(value, axis, pairs)


def spread(grad_iface):
    return jnp.pad(grad_iface, ((0, 0), (0, 1), (0, 0))) - jnp.pad(
        grad_iface, ((0, 0), (1, 0), (0, 0))
    )


def spread0(grad_iface):
    return pad_sum(grad_iface, 0, -1.0)


def pad_sum(grad_iface, axis, sign=1.0):
    pads = [(0, 0)] * grad_iface.ndim
    low, high = list(pads), list(pads)
    low[axis], high[axis] = (0, 1), (1, 0)
    if sign < 0:
        return jnp.pad(grad_iface, low) - jnp.pad(grad_iface, high)
    return jnp.pad(grad_iface, low) + jnp.pad(grad_iface, high)


def split2(x):
    hi = lax.reduce_precision(x, exponent_bits=8, mantissa_bits=7)
    lo = x - hi
    return jnp.concatenate([hi.astype(jnp.bfloat16), lo.astype(jnp.bfloat16)])


def exact_select(rows, select, contract):
    n = rows.shape[0]
    parts = lax.dot_general(
        split2(rows),
        select,
        (((1,), (contract,)), ((), ())),
        preferred_element_type=jnp.float32,
    )
    return parts[:n] + parts[n:]


def reduce_scatter(value, axis):
    size = lax.axis_size(axis)
    index = lax.axis_index(axis)
    width = value.shape[-1] // size
    cur = value.reshape(value.shape[:-1] + (size, width))
    dist = size // 2
    while dist >= 1:
        half = cur.shape[-2] // 2
        lower, upper = cur[..., :half, :], cur[..., half:, :]
        bit = (index // dist) % 2 == 1
        keep = jnp.where(bit, upper, lower)
        send = jnp.where(bit, lower, upper)
        cur = keep + from_partner(send, axis, dist)
        dist //= 2
    return cur.reshape(value.shape[:-1] + (width,))


def sum_scatter(value, axis):
    size = lax.axis_size(axis)
    width = value.shape[-1] // size
    parts = jnp.moveaxis(value.reshape(value.shape[:-1] + (size, width)), -2, 0)
    got = lax.all_to_all(parts, axis, 0, 0, tiled=True)
    return jnp.sum(got, axis=0)


def body(
    pressure,
    heat,
    log_cond,
    log_therm,
    frozen,
    frozen_flag,
    recharge,
    face_cols,
    face_weight,
    cot_pressure,
    cot_heat,
):
    members, layers, width = pressure.shape
    rounds, face = face_cols.shape
    p_old = pressure.transpose(1, 0, 2)
    t_old = heat.transpose(1, 0, 2)
    c_p = cot_pressure.transpose(1, 0, 2)
    c_t = cot_heat.transpose(1, 0, 2)
    blocked = frozen * frozen_flag.astype(jnp.float32)
    cond = jnp.exp(log_cond - 3.0 * blocked)
    therm = jnp.exp(log_therm) * (1.0 + blocked)
    g_p = 0.1 * c_p
    g_t = 0.1 * c_t

    cols = face_cols.reshape(rounds * face)
    select = (cols[:, None] == jnp.arange(width, dtype=jnp.int32)[None, :]).astype(
        jnp.bfloat16
    )

    n_field = members * layers
    rows = jnp.concatenate(
        [
            jnp.stack([p_old, t_old, c_p, c_t]).reshape(4 * n_field, width),
            jnp.stack([cond, therm]).reshape(2 * layers, width),
        ]
    )
    picked = exact_select(rows, select, 1)
    fields_f = picked[: 4 * n_field].reshape(4, layers, members, rounds, face)
    coefs_f = picked[4 * n_field :].reshape(2, layers, 1, rounds, face)
    wc = face_weight * coefs_f
    own = fields_f[:2]
    g_f = 0.1 * fields_f[2:]
    g_own = g_f * wc
    sending = jnp.concatenate([own, g_own])

    far = []
    for index in range(rounds):
        far.append(from_partner(sending[..., index, :], "space", 1 << index))
    far = jnp.stack(far, axis=-2)

    diff = far[:2] - own
    update = wc * diff
    adj_lat = far[2:] - g_own
    param_lat = face_weight * jnp.sum(g_f * diff, axis=2)

    kf = (0.5 * (cond[:-1] + cond[1:]))[:, None]
    kt = (0.5 * (therm[:-1] + therm[1:]))[:, None]
    d_p = p_old[1:] - p_old[:-1]
    d_t = t_old[1:] - t_old[:-1]
    flow = kf * d_p
    conduct = kt * d_t
    t_mean = 0.5 * (t_old[:-1] + t_old[1:])
    carried = flow * t_mean
    da = g_p[:-1] - g_p[1:]
    db = g_t[:-1] - g_t[1:]
    g_carried = 0.5 * db
    g_flow = da + g_carried * t_mean
    g_kf = jnp.sum(g_flow * d_p, axis=1)
    g_kt = jnp.sum(db * d_t, axis=1)
    vert_grads = jnp.stack([0.5 * pad_sum(g_kf, 0), 0.5 * pad_sum(g_kt, 0)])

    lat_grads = exact_select(
        param_lat.reshape(2 * layers, rounds * face), select, 0
    ).reshape(2, layers, width)
    grads = (vert_grads + lat_grads) * jnp.stack([cond, therm])
    owned = sum_scatter(grads, "member")

    lat = exact_select(
        jnp.concatenate([update, adj_lat]).reshape(4 * n_field, rounds * face),
        select,
        0,
    ).reshape(4, layers, members, width)

    p_rate = spread0(flow)
    p_rate = p_rate.at[0].add(recharge)
    t_rate = spread0(conduct) + 0.5 * spread0(carried)
    new_pressure = p_old + 0.1 * (p_rate + lat[0])
    new_heat = t_old + 0.1 * (t_rate + lat[1])
    adj_pressure = c_p - spread0(g_flow * kf) + lat[2]
    adj_heat = c_t - spread0(db * kt) + 0.5 * pad_sum(g_carried * flow, 0) + lat[3]
    outs = [new_pressure, new_heat, adj_pressure, adj_heat]
    return tuple(o.transpose(1, 0, 2) for o in outs) + (owned,)


def solution(mesh):
    placed = (
        P("member", None, "space"),
        P("member", None, "space"),
        P(None, "space"),
        P(None, "space"),
        P(None, "space"),
        P(None, "space"),
        P("member", "space"),
        P(None, "space"),
        P(None, "space"),
        P("member", None, "space"),
        P("member", None, "space"),
    )
    return jax.shard_map(
        body,
        mesh=mesh,
        in_specs=placed,
        out_specs=(
            P("member", None, "space"),
            P("member", None, "space"),
            P("member", None, "space"),
            P("member", None, "space"),
            P(None, None, ("space", "member")),
        ),
        check_vma=False,
    )
```

```python
import jax
import jax.numpy as jnp
from jax import lax
from jax.sharding import PartitionSpec as P


def from_partner(value, axis, mask):
    pairs = [(source, source ^ mask) for source in range(lax.axis_size(axis))]
    return lax.ppermute(value, axis, pairs)


def spread(grad_iface):
    return jnp.pad(grad_iface, ((0, 0), (0, 1), (0, 0))) - jnp.pad(
        grad_iface, ((0, 0), (1, 0), (0, 0))
    )


def spread0(grad_iface):
    return pad_sum(grad_iface, 0, -1.0)


def pad_sum(grad_iface, axis, sign=1.0):
    pads = [(0, 0)] * grad_iface.ndim
    low, high = list(pads), list(pads)
    low[axis], high[axis] = (0, 1), (1, 0)
    if sign < 0:
        return jnp.pad(grad_iface, low) - jnp.pad(grad_iface, high)
    return jnp.pad(grad_iface, low) + jnp.pad(grad_iface, high)


def split2(x):
    hi = lax.reduce_precision(x, exponent_bits=8, mantissa_bits=7)
    lo = x - hi
    return jnp.concatenate([hi.astype(jnp.bfloat16), lo.astype(jnp.bfloat16)])


def exact_select(rows, select, contract):
    n = rows.shape[0]
    parts = lax.dot_general(
        split2(rows),
        select,
        (((1,), (contract,)), ((), ())),
        preferred_element_type=jnp.float32,
    )
    return parts[:n] + parts[n:]


def reduce_scatter(value, axis):
    size = lax.axis_size(axis)
    index = lax.axis_index(axis)
    width = value.shape[-1] // size
    cur = value.reshape(value.shape[:-1] + (size, width))
    dist = size // 2
    while dist >= 1:
        half = cur.shape[-2] // 2
        lower, upper = cur[..., :half, :], cur[..., half:, :]
        bit = (index // dist) % 2 == 1
        keep = jnp.where(bit, upper, lower)
        send = jnp.where(bit, lower, upper)
        cur = keep + from_partner(send, axis, dist)
        dist //= 2
    return cur.reshape(value.shape[:-1] + (width,))


def sum_scatter(value, axis):
    size = lax.axis_size(axis)
    width = value.shape[-1] // size
    parts = jnp.moveaxis(value.reshape(value.shape[:-1] + (size, width)), -2, 0)
    got = lax.all_to_all(parts, axis, 0, 0, tiled=True)
    total = got[0]
    for index in range(1, size):
        total = total + got[index]
    return total


def body(
    pressure,
    heat,
    log_cond,
    log_therm,
    frozen,
    frozen_flag,
    recharge,
    face_cols,
    face_weight,
    cot_pressure,
    cot_heat,
):
    members, layers, width = pressure.shape
    rounds, face = face_cols.shape
    p_old = pressure.transpose(1, 0, 2)
    t_old = heat.transpose(1, 0, 2)
    c_p = cot_pressure.transpose(1, 0, 2)
    c_t = cot_heat.transpose(1, 0, 2)
    blocked = frozen * frozen_flag.astype(jnp.float32)
    cond = jnp.exp(log_cond - 3.0 * blocked)
    therm = jnp.exp(log_therm) * (1.0 + blocked)
    g_p = 0.1 * c_p
    g_t = 0.1 * c_t

    cols = face_cols.reshape(rounds * face)
    select = (cols[:, None] == jnp.arange(width, dtype=jnp.int32)[None, :]).astype(
        jnp.bfloat16
    )

    n_field = members * layers
    rows = jnp.concatenate(
        [
            jnp.stack([p_old, t_old, c_p, c_t]).reshape(4 * n_field, width),
            jnp.stack([cond, therm]).reshape(2 * layers, width),
        ]
    )
    picked = exact_select(rows, select, 1)
    fields_f = picked[: 4 * n_field].reshape(4, layers, members, rounds, face)
    coefs_f = picked[4 * n_field :].reshape(2, layers, 1, rounds, face)
    wc = face_weight * coefs_f
    own = fields_f[:2]
    g_f = 0.1 * fields_f[2:]
    g_own = g_f * wc
    sending = jnp.concatenate([own, g_own])

    far = []
    for index in range(rounds):
        far.append(from_partner(sending[..., index, :], "space", 1 << index))
    far = jnp.stack(far, axis=-2)

    diff = far[:2] - own
    update = wc * diff
    adj_lat = far[2:] - g_own
    param_lat = face_weight * jnp.sum(g_f * diff, axis=2)

    kf = (0.5 * (cond[:-1] + cond[1:]))[:, None]
    kt = (0.5 * (therm[:-1] + therm[1:]))[:, None]
    d_p = p_old[1:] - p_old[:-1]
    d_t = t_old[1:] - t_old[:-1]
    flow = kf * d_p
    conduct = kt * d_t
    t_mean = 0.5 * (t_old[:-1] + t_old[1:])
    carried = flow * t_mean
    da = g_p[:-1] - g_p[1:]
    db = g_t[:-1] - g_t[1:]
    g_carried = 0.5 * db
    g_flow = da + g_carried * t_mean
    g_kf = jnp.sum(g_flow * d_p, axis=1)
    g_kt = jnp.sum(db * d_t, axis=1)
    vert_grads = jnp.stack([0.5 * pad_sum(g_kf, 0), 0.5 * pad_sum(g_kt, 0)])

    placed = exact_select(
        jnp.concatenate(
            [
                param_lat.reshape(2 * layers, rounds * face),
                jnp.concatenate([update, adj_lat]).reshape(4 * n_field, rounds * face),
            ]
        ),
        select,
        0,
    )
    lat_grads = placed[: 2 * layers].reshape(2, layers, width)
    lat = placed[2 * layers :].reshape(4, layers, members, width)
    grads = (vert_grads + lat_grads) * jnp.stack([cond, therm])
    owned = sum_scatter(grads, "member")


    p_rate = spread0(flow)
    p_rate = p_rate.at[0].add(recharge)
    t_rate = spread0(conduct) + 0.5 * spread0(carried)
    new_pressure = p_old + 0.1 * (p_rate + lat[0])
    new_heat = t_old + 0.1 * (t_rate + lat[1])
    adj_pressure = c_p - spread0(g_flow * kf) + lat[2]
    adj_heat = c_t - spread0(db * kt) + 0.5 * pad_sum(g_carried * flow, 0) + lat[3]
    outs = [new_pressure, new_heat, adj_pressure, adj_heat]
    return tuple(o.transpose(1, 0, 2) for o in outs) + (owned,)


def solution(mesh):
    placed = (
        P("member", None, "space"),
        P("member", None, "space"),
        P(None, "space"),
        P(None, "space"),
        P(None, "space"),
        P(None, "space"),
        P("member", "space"),
        P(None, "space"),
        P(None, "space"),
        P("member", None, "space"),
        P("member", None, "space"),
    )
    return jax.shard_map(
        body,
        mesh=mesh,
        in_specs=placed,
        out_specs=(
            P("member", None, "space"),
            P("member", None, "space"),
            P("member", None, "space"),
            P("member", None, "space"),
            P(None, None, ("space", "member")),
        ),
        check_vma=False,
    )
```

```python
import jax
import jax.numpy as jnp
from jax import lax
from jax.sharding import PartitionSpec as P


def from_partner(value, axis, mask):
    pairs = [(source, source ^ mask) for source in range(lax.axis_size(axis))]
    return lax.ppermute(value, axis, pairs)


def spread(grad_iface):
    return jnp.pad(grad_iface, ((0, 0), (0, 1), (0, 0))) - jnp.pad(
        grad_iface, ((0, 0), (1, 0), (0, 0))
    )


def spread0(grad_iface):
    return pad_sum(grad_iface, 0, -1.0)


def pad_sum(grad_iface, axis, sign=1.0):
    pads = [(0, 0)] * grad_iface.ndim
    low, high = list(pads), list(pads)
    low[axis], high[axis] = (0, 1), (1, 0)
    if sign < 0:
        return jnp.pad(grad_iface, low) - jnp.pad(grad_iface, high)
    return jnp.pad(grad_iface, low) + jnp.pad(grad_iface, high)


def split2(x):
    hi = lax.reduce_precision(x, exponent_bits=8, mantissa_bits=7)
    lo = x - hi
    return jnp.concatenate([hi.astype(jnp.bfloat16), lo.astype(jnp.bfloat16)])


def exact_select(rows, select, contract):
    n = rows.shape[0]
    parts = lax.dot_general(
        split2(rows),
        select,
        (((1,), (contract,)), ((), ())),
        preferred_element_type=jnp.float32,
    )
    return parts[:n] + parts[n:]


def reduce_scatter(value, axis):
    size = lax.axis_size(axis)
    index = lax.axis_index(axis)
    width = value.shape[-1] // size
    cur = value.reshape(value.shape[:-1] + (size, width))
    dist = size // 2
    while dist >= 1:
        half = cur.shape[-2] // 2
        lower, upper = cur[..., :half, :], cur[..., half:, :]
        bit = (index // dist) % 2 == 1
        keep = jnp.where(bit, upper, lower)
        send = jnp.where(bit, lower, upper)
        cur = keep + from_partner(send, axis, dist)
        dist //= 2
    return cur.reshape(value.shape[:-1] + (width,))


def sum_scatter(value, axis):
    size = lax.axis_size(axis)
    width = value.shape[-1] // size
    parts = jnp.moveaxis(value.reshape(value.shape[:-1] + (size, width)), -2, 0)
    got = lax.all_to_all(parts, axis, 0, 0, tiled=True)
    total = got[0]
    for index in range(1, size):
        total = total + got[index]
    return total


def body(
    pressure,
    heat,
    log_cond,
    log_therm,
    frozen,
    frozen_flag,
    recharge,
    face_cols,
    face_weight,
    cot_pressure,
    cot_heat,
):
    members, layers, width = pressure.shape
    rounds, face = face_cols.shape
    p_old = pressure.transpose(1, 0, 2)
    t_old = heat.transpose(1, 0, 2)
    c_p = cot_pressure.transpose(1, 0, 2)
    c_t = cot_heat.transpose(1, 0, 2)
    blocked = frozen * frozen_flag.astype(jnp.float32)
    cond = jnp.exp(log_cond - 3.0 * blocked)
    therm = jnp.exp(log_therm) * (1.0 + blocked)
    g_p = 0.1 * c_p
    g_t = 0.1 * c_t

    cols = face_cols.reshape(rounds * face)
    select = (cols[:, None] == jnp.arange(width, dtype=jnp.int32)[None, :]).astype(
        jnp.bfloat16
    )

    n_field = members * layers
    pieces = [x.reshape(n_field, width) for x in (p_old, t_old, c_p, c_t)]
    pieces += [cond, therm]
    highs = [lax.reduce_precision(x, exponent_bits=8, mantissa_bits=7) for x in pieces]
    lows = [x - h for x, h in zip(pieces, highs)]
    row_parts = jnp.concatenate([x.astype(jnp.bfloat16) for x in highs + lows])
    picked = lax.dot_general(
        row_parts, select, (((1,), (1,)), ((), ())), preferred_element_type=jnp.float32
    )
    picked = picked[: picked.shape[0] // 2] + picked[picked.shape[0] // 2 :]
    fields_f = picked[: 4 * n_field].reshape(4, layers, members, rounds, face)
    coefs_f = picked[4 * n_field :].reshape(2, layers, 1, rounds, face)
    wc = face_weight * coefs_f
    own = fields_f[:2]
    g_f = 0.1 * fields_f[2:]
    g_own = g_f * wc
    sending = jnp.concatenate([own, g_own])

    far = []
    for index in range(rounds):
        far.append(from_partner(sending[..., index, :], "space", 1 << index))
    far = jnp.stack(far, axis=-2)

    diff = far[:2] - own
    update = wc * diff
    adj_lat = far[2:] - g_own
    param_lat = face_weight * jnp.sum(g_f * diff, axis=2)

    kf = (0.5 * (cond[:-1] + cond[1:]))[:, None]
    kt = (0.5 * (therm[:-1] + therm[1:]))[:, None]
    d_p = p_old[1:] - p_old[:-1]
    d_t = t_old[1:] - t_old[:-1]
    flow = kf * d_p
    conduct = kt * d_t
    t_mean = 0.5 * (t_old[:-1] + t_old[1:])
    carried = flow * t_mean
    da = g_p[:-1] - g_p[1:]
    db = g_t[:-1] - g_t[1:]
    g_carried = 0.5 * db
    g_flow = da + g_carried * t_mean
    g_kf = jnp.sum(g_flow * d_p, axis=1)
    g_kt = jnp.sum(db * d_t, axis=1)
    vert_grads = jnp.stack([0.5 * pad_sum(g_kf, 0), 0.5 * pad_sum(g_kt, 0)])

    placed = exact_select(
        jnp.concatenate(
            [
                param_lat.reshape(2 * layers, rounds * face),
                jnp.concatenate([update, adj_lat]).reshape(4 * n_field, rounds * face),
            ]
        ),
        select,
        0,
    )
    lat_grads = placed[: 2 * layers].reshape(2, layers, width)
    lat = placed[2 * layers :].reshape(4, layers, members, width)
    grads = (vert_grads + lat_grads) * jnp.stack([cond, therm])
    owned = sum_scatter(grads, "member")


    p_rate = spread0(flow)
    p_rate = p_rate.at[0].add(recharge)
    t_rate = spread0(conduct) + 0.5 * spread0(carried)
    new_pressure = p_old + 0.1 * (p_rate + lat[0])
    new_heat = t_old + 0.1 * (t_rate + lat[1])
    adj_pressure = c_p - spread0(g_flow * kf) + lat[2]
    adj_heat = c_t - spread0(db * kt) + 0.5 * pad_sum(g_carried * flow, 0) + lat[3]
    outs = [new_pressure, new_heat, adj_pressure, adj_heat]
    return tuple(o.transpose(1, 0, 2) for o in outs) + (owned,)


def solution(mesh):
    placed = (
        P("member", None, "space"),
        P("member", None, "space"),
        P(None, "space"),
        P(None, "space"),
        P(None, "space"),
        P(None, "space"),
        P("member", "space"),
        P(None, "space"),
        P(None, "space"),
        P("member", None, "space"),
        P("member", None, "space"),
    )
    return jax.shard_map(
        body,
        mesh=mesh,
        in_specs=placed,
        out_specs=(
            P("member", None, "space"),
            P("member", None, "space"),
            P("member", None, "space"),
            P("member", None, "space"),
            P(None, None, ("space", "member")),
        ),
        check_vma=False,
    )
```

```python
import jax
import jax.numpy as jnp
from jax import lax
from jax.sharding import PartitionSpec as P


def from_partner(value, axis, mask):
    pairs = [(source, source ^ mask) for source in range(lax.axis_size(axis))]
    return lax.ppermute(value, axis, pairs)


def spread(grad_iface):
    return jnp.pad(grad_iface, ((0, 0), (0, 1), (0, 0))) - jnp.pad(
        grad_iface, ((0, 0), (1, 0), (0, 0))
    )


def spread0(grad_iface):
    return pad_sum(grad_iface, 0, -1.0)


def pad_sum(grad_iface, axis, sign=1.0):
    pads = [(0, 0)] * grad_iface.ndim
    low, high = list(pads), list(pads)
    low[axis], high[axis] = (0, 1), (1, 0)
    if sign < 0:
        return jnp.pad(grad_iface, low) - jnp.pad(grad_iface, high)
    return jnp.pad(grad_iface, low) + jnp.pad(grad_iface, high)


def split2(x):
    hi = lax.reduce_precision(x, exponent_bits=8, mantissa_bits=7)
    lo = x - hi
    return jnp.concatenate([hi.astype(jnp.bfloat16), lo.astype(jnp.bfloat16)])


def exact_select(rows, select, contract):
    n = rows.shape[0]
    parts = lax.dot_general(
        split2(rows),
        select,
        (((1,), (contract,)), ((), ())),
        preferred_element_type=jnp.float32,
    )
    return parts[:n] + parts[n:]


def reduce_scatter(value, axis):
    size = lax.axis_size(axis)
    index = lax.axis_index(axis)
    width = value.shape[-1] // size
    cur = value.reshape(value.shape[:-1] + (size, width))
    dist = size // 2
    while dist >= 1:
        half = cur.shape[-2] // 2
        lower, upper = cur[..., :half, :], cur[..., half:, :]
        bit = (index // dist) % 2 == 1
        keep = jnp.where(bit, upper, lower)
        send = jnp.where(bit, lower, upper)
        cur = keep + from_partner(send, axis, dist)
        dist //= 2
    return cur.reshape(value.shape[:-1] + (width,))


def sum_scatter(value, axis):
    size = lax.axis_size(axis)
    width = value.shape[-1] // size
    rows = value.reshape(-1, size, width)
    parts = jnp.moveaxis(rows, 1, 0)
    got = lax.all_to_all(parts, axis, 0, 0, tiled=True)
    total = got[0]
    for index in range(1, size):
        total = total + got[index]
    return total.reshape(value.shape[:-1] + (width,))


def body(
    pressure,
    heat,
    log_cond,
    log_therm,
    frozen,
    frozen_flag,
    recharge,
    face_cols,
    face_weight,
    cot_pressure,
    cot_heat,
):
    members, layers, width = pressure.shape
    rounds, face = face_cols.shape
    p_old = pressure.transpose(1, 0, 2)
    t_old = heat.transpose(1, 0, 2)
    c_p = cot_pressure.transpose(1, 0, 2)
    c_t = cot_heat.transpose(1, 0, 2)
    blocked = frozen * frozen_flag.astype(jnp.float32)
    cond = jnp.exp(log_cond - 3.0 * blocked)
    therm = jnp.exp(log_therm) * (1.0 + blocked)
    g_p = 0.1 * c_p
    g_t = 0.1 * c_t

    cols = face_cols.reshape(rounds * face)
    select = (cols[:, None] == jnp.arange(width, dtype=jnp.int32)[None, :]).astype(
        jnp.bfloat16
    )

    n_field = members * layers
    rows = jnp.concatenate(
        [
            jnp.stack([p_old, t_old, c_p, c_t]).reshape(4 * n_field, width),
            jnp.stack([cond, therm]).reshape(2 * layers, width),
        ]
    )
    picked = exact_select(rows, select, 1)
    fields_f = picked[: 4 * n_field].reshape(4, layers, members, rounds, face)
    coefs_f = picked[4 * n_field :].reshape(2, layers, 1, rounds, face)
    wc = face_weight * coefs_f
    own = fields_f[:2]
    g_f = 0.1 * fields_f[2:]
    g_own = g_f * wc
    sending = jnp.concatenate([own, g_own])

    far = []
    for index in range(rounds):
        far.append(from_partner(sending[..., index, :], "space", 1 << index))
    far = jnp.stack(far, axis=-2)

    diff = far[:2] - own
    update = wc * diff
    adj_lat = far[2:] - g_own
    param_lat = face_weight * jnp.sum(g_f * diff, axis=2)

    kf = (0.5 * (cond[:-1] + cond[1:]))[:, None]
    kt = (0.5 * (therm[:-1] + therm[1:]))[:, None]
    d_p = p_old[1:] - p_old[:-1]
    d_t = t_old[1:] - t_old[:-1]
    flow = kf * d_p
    conduct = kt * d_t
    t_mean = 0.5 * (t_old[:-1] + t_old[1:])
    carried = flow * t_mean
    da = g_p[:-1] - g_p[1:]
    db = g_t[:-1] - g_t[1:]
    g_carried = 0.5 * db
    g_flow = da + g_carried * t_mean
    g_kf = jnp.sum(g_flow * d_p, axis=1)
    g_kt = jnp.sum(db * d_t, axis=1)
    vert_grads = jnp.stack([0.5 * pad_sum(g_kf, 0), 0.5 * pad_sum(g_kt, 0)])

    placed = exact_select(
        jnp.concatenate(
            [
                param_lat.reshape(2 * layers, rounds * face),
                jnp.concatenate([update, adj_lat]).reshape(4 * n_field, rounds * face),
            ]
        ),
        select,
        0,
    )
    lat_grads = placed[: 2 * layers].reshape(2, layers, width)
    lat = placed[2 * layers :].reshape(4, layers, members, width)
    grads = (vert_grads + lat_grads) * jnp.stack([cond, therm])
    owned = sum_scatter(grads, "member")


    p_rate = spread0(flow)
    p_rate = p_rate.at[0].add(recharge)
    t_rate = spread0(conduct) + 0.5 * spread0(carried)
    new_pressure = p_old + 0.1 * (p_rate + lat[0])
    new_heat = t_old + 0.1 * (t_rate + lat[1])
    adj_pressure = c_p - spread0(g_flow * kf) + lat[2]
    adj_heat = c_t - spread0(db * kt) + 0.5 * pad_sum(g_carried * flow, 0) + lat[3]
    outs = [new_pressure, new_heat, adj_pressure, adj_heat]
    return tuple(o.transpose(1, 0, 2) for o in outs) + (owned,)


def solution(mesh):
    placed = (
        P("member", None, "space"),
        P("member", None, "space"),
        P(None, "space"),
        P(None, "space"),
        P(None, "space"),
        P(None, "space"),
        P("member", "space"),
        P(None, "space"),
        P(None, "space"),
        P("member", None, "space"),
        P("member", None, "space"),
    )
    return jax.shard_map(
        body,
        mesh=mesh,
        in_specs=placed,
        out_specs=(
            P("member", None, "space"),
            P("member", None, "space"),
            P("member", None, "space"),
            P("member", None, "space"),
            P(None, None, ("space", "member")),
        ),
        check_vma=False,
    )
```

```python
import jax
import jax.numpy as jnp
from jax import lax
from jax.sharding import PartitionSpec as P


def from_partner(value, axis, mask):
    pairs = [(source, source ^ mask) for source in range(lax.axis_size(axis))]
    return lax.ppermute(value, axis, pairs)


def spread(grad_iface):
    return jnp.pad(grad_iface, ((0, 0), (0, 1), (0, 0))) - jnp.pad(
        grad_iface, ((0, 0), (1, 0), (0, 0))
    )


def spread0(grad_iface):
    return pad_sum(grad_iface, 0, -1.0)


def pad_sum(grad_iface, axis, sign=1.0):
    pads = [(0, 0)] * grad_iface.ndim
    low, high = list(pads), list(pads)
    low[axis], high[axis] = (0, 1), (1, 0)
    if sign < 0:
        return jnp.pad(grad_iface, low) - jnp.pad(grad_iface, high)
    return jnp.pad(grad_iface, low) + jnp.pad(grad_iface, high)


def split2(x):
    hi = lax.reduce_precision(x, exponent_bits=8, mantissa_bits=7)
    lo = x - hi
    return jnp.concatenate([hi.astype(jnp.bfloat16), lo.astype(jnp.bfloat16)])


def exact_select(rows, select, contract):
    n = rows.shape[0]
    parts = lax.dot_general(
        split2(rows),
        select,
        (((1,), (contract,)), ((), ())),
        preferred_element_type=jnp.float32,
    )
    return parts[:n] + parts[n:]


def reduce_scatter(value, axis):
    size = lax.axis_size(axis)
    index = lax.axis_index(axis)
    width = value.shape[-1] // size
    cur = value.reshape(value.shape[:-1] + (size, width))
    dist = size // 2
    while dist >= 1:
        half = cur.shape[-2] // 2
        lower, upper = cur[..., :half, :], cur[..., half:, :]
        bit = (index // dist) % 2 == 1
        keep = jnp.where(bit, upper, lower)
        send = jnp.where(bit, lower, upper)
        cur = keep + from_partner(send, axis, dist)
        dist //= 2
    return cur.reshape(value.shape[:-1] + (width,))


def sum_scatter(value, axis):
    size = lax.axis_size(axis)
    width = value.shape[-1] // size
    parts = jnp.moveaxis(value.reshape(value.shape[:-1] + (size, width)), -2, 0)
    got = lax.all_to_all(parts, axis, 0, 0, tiled=True)
    total = got[0]
    for index in range(1, size):
        total = total + got[index]
    return total


def body(
    pressure,
    heat,
    log_cond,
    log_therm,
    frozen,
    frozen_flag,
    recharge,
    face_cols,
    face_weight,
    cot_pressure,
    cot_heat,
):
    members, layers, width = pressure.shape
    rounds, face = face_cols.shape
    p_old = pressure.transpose(1, 0, 2)
    t_old = heat.transpose(1, 0, 2)
    c_p = cot_pressure.transpose(1, 0, 2)
    c_t = cot_heat.transpose(1, 0, 2)
    blocked = frozen * frozen_flag.astype(jnp.float32)
    cond = jnp.exp(log_cond - 3.0 * blocked)
    therm = jnp.exp(log_therm) * (1.0 + blocked)
    g_p = 0.1 * c_p
    g_t = 0.1 * c_t

    order = [2, 3, 0, 1] if rounds == 4 else list(range(rounds))
    face_cols = jnp.concatenate([face_cols[i : i + 1] for i in order])
    face_weight = jnp.concatenate([face_weight[i : i + 1] for i in order])
    cols = face_cols.reshape(rounds * face)
    select = (cols[:, None] == jnp.arange(width, dtype=jnp.int32)[None, :]).astype(
        jnp.bfloat16
    )

    n_field = members * layers
    rows = jnp.concatenate(
        [
            jnp.stack([p_old, t_old, c_p, c_t]).reshape(4 * n_field, width),
            jnp.stack([cond, therm]).reshape(2 * layers, width),
        ]
    )
    picked = exact_select(rows, select, 1)
    fields_f = picked[: 4 * n_field].reshape(4, layers, members, rounds, face)
    coefs_f = picked[4 * n_field :].reshape(2, layers, 1, rounds, face)
    wc = face_weight * coefs_f
    own = fields_f[:2]
    g_f = 0.1 * fields_f[2:]
    g_own = g_f * wc
    sending = jnp.concatenate([own, g_own])

    far = []
    for index in range(rounds):
        far.append(from_partner(sending[..., index, :], "space", 1 << order[index]))
    far = jnp.stack(far, axis=-2)

    diff = far[:2] - own
    update = wc * diff
    adj_lat = far[2:] - g_own
    param_lat = face_weight * jnp.sum(g_f * diff, axis=2)

    kf = (0.5 * (cond[:-1] + cond[1:]))[:, None]
    kt = (0.5 * (therm[:-1] + therm[1:]))[:, None]
    d_p = p_old[1:] - p_old[:-1]
    d_t = t_old[1:] - t_old[:-1]
    flow = kf * d_p
    conduct = kt * d_t
    t_mean = 0.5 * (t_old[:-1] + t_old[1:])
    carried = flow * t_mean
    da = g_p[:-1] - g_p[1:]
    db = g_t[:-1] - g_t[1:]
    g_carried = 0.5 * db
    g_flow = da + g_carried * t_mean
    g_kf = jnp.sum(g_flow * d_p, axis=1)
    g_kt = jnp.sum(db * d_t, axis=1)
    vert_grads = jnp.stack([0.5 * pad_sum(g_kf, 0), 0.5 * pad_sum(g_kt, 0)])

    placed = exact_select(
        jnp.concatenate(
            [
                param_lat.reshape(2 * layers, rounds * face),
                jnp.concatenate([update, adj_lat]).reshape(4 * n_field, rounds * face),
            ]
        ),
        select,
        0,
    )
    lat_grads = placed[: 2 * layers].reshape(2, layers, width)
    lat = placed[2 * layers :].reshape(4, layers, members, width)
    grads = (vert_grads + lat_grads) * jnp.stack([cond, therm])
    owned = sum_scatter(grads, "member")


    p_rate = spread0(flow)
    p_rate = p_rate.at[0].add(recharge)
    t_rate = spread0(conduct) + 0.5 * spread0(carried)
    new_pressure = p_old + 0.1 * (p_rate + lat[0])
    new_heat = t_old + 0.1 * (t_rate + lat[1])
    adj_pressure = c_p - spread0(g_flow * kf) + lat[2]
    adj_heat = c_t - spread0(db * kt) + 0.5 * pad_sum(g_carried * flow, 0) + lat[3]
    outs = [new_pressure, new_heat, adj_pressure, adj_heat]
    return tuple(o.transpose(1, 0, 2) for o in outs) + (owned,)


def solution(mesh):
    placed = (
        P("member", None, "space"),
        P("member", None, "space"),
        P(None, "space"),
        P(None, "space"),
        P(None, "space"),
        P(None, "space"),
        P("member", "space"),
        P(None, "space"),
        P(None, "space"),
        P("member", None, "space"),
        P("member", None, "space"),
    )
    return jax.shard_map(
        body,
        mesh=mesh,
        in_specs=placed,
        out_specs=(
            P("member", None, "space"),
            P("member", None, "space"),
            P("member", None, "space"),
            P("member", None, "space"),
            P(None, None, ("space", "member")),
        ),
        check_vma=False,
    )
```

```python
import jax
import jax.numpy as jnp
from jax import lax
from jax.sharding import PartitionSpec as P


def from_partner(value, axis, mask):
    pairs = [(source, source ^ mask) for source in range(lax.axis_size(axis))]
    return lax.ppermute(value, axis, pairs)


def spread(grad_iface):
    return jnp.pad(grad_iface, ((0, 0), (0, 1), (0, 0))) - jnp.pad(
        grad_iface, ((0, 0), (1, 0), (0, 0))
    )


def spread0(grad_iface):
    return pad_sum(grad_iface, 0, -1.0)


def pad_sum(grad_iface, axis, sign=1.0):
    pads = [(0, 0)] * grad_iface.ndim
    low, high = list(pads), list(pads)
    low[axis], high[axis] = (0, 1), (1, 0)
    if sign < 0:
        return jnp.pad(grad_iface, low) - jnp.pad(grad_iface, high)
    return jnp.pad(grad_iface, low) + jnp.pad(grad_iface, high)


def split2(x):
    hi = lax.reduce_precision(x, exponent_bits=8, mantissa_bits=7)
    lo = x - hi
    return jnp.concatenate([hi.astype(jnp.bfloat16), lo.astype(jnp.bfloat16)])


def exact_select(rows, select, contract):
    n = rows.shape[0]
    parts = lax.dot_general(
        split2(rows),
        select,
        (((1,), (contract,)), ((), ())),
        preferred_element_type=jnp.float32,
    )
    return parts[:n] + parts[n:]


def reduce_scatter(value, axis):
    size = lax.axis_size(axis)
    index = lax.axis_index(axis)
    width = value.shape[-1] // size
    cur = value.reshape(value.shape[:-1] + (size, width))
    dist = size // 2
    while dist >= 1:
        half = cur.shape[-2] // 2
        lower, upper = cur[..., :half, :], cur[..., half:, :]
        bit = (index // dist) % 2 == 1
        keep = jnp.where(bit, upper, lower)
        send = jnp.where(bit, lower, upper)
        cur = keep + from_partner(send, axis, dist)
        dist //= 2
    return cur.reshape(value.shape[:-1] + (width,))


def sum_scatter(value, axis):
    size = lax.axis_size(axis)
    width = value.shape[-1] // size
    parts = jnp.moveaxis(value.reshape(value.shape[:-1] + (size, width)), -2, 0)
    got = lax.all_to_all(parts, axis, 0, 0, tiled=True)
    total = got[0]
    for index in range(1, size):
        total = total + got[index]
    return total


def body(
    pressure,
    heat,
    log_cond,
    log_therm,
    frozen,
    frozen_flag,
    recharge,
    face_cols,
    face_weight,
    cot_pressure,
    cot_heat,
):
    members, layers, width = pressure.shape
    rounds, face = face_cols.shape
    p_old = pressure.transpose(1, 0, 2)
    t_old = heat.transpose(1, 0, 2)
    c_p = cot_pressure.transpose(1, 0, 2)
    c_t = cot_heat.transpose(1, 0, 2)
    blocked = frozen * frozen_flag.astype(jnp.float32)
    cond = jnp.exp(log_cond - 3.0 * blocked)
    therm = jnp.exp(log_therm) * (1.0 + blocked)
    g_p = 0.1 * c_p
    g_t = 0.1 * c_t

    order = [2, 3, 1, 0] if rounds == 4 else list(range(rounds))
    face_cols = jnp.concatenate([face_cols[i : i + 1] for i in order])
    face_weight = jnp.concatenate([face_weight[i : i + 1] for i in order])
    cols = face_cols.reshape(rounds * face)
    select = (cols[:, None] == jnp.arange(width, dtype=jnp.int32)[None, :]).astype(
        jnp.bfloat16
    )

    n_field = members * layers
    rows = jnp.concatenate(
        [
            jnp.stack([p_old, t_old, c_p, c_t]).reshape(4 * n_field, width),
            jnp.stack([cond, therm]).reshape(2 * layers, width),
        ]
    )
    picked = exact_select(rows, select, 1)
    fields_f = picked[: 4 * n_field].reshape(4, layers, members, rounds, face)
    coefs_f = picked[4 * n_field :].reshape(2, layers, 1, rounds, face)
    wc = face_weight * coefs_f
    own = fields_f[:2]
    g_f = 0.1 * fields_f[2:]
    g_own = g_f * wc
    sending = jnp.concatenate([own, g_own])

    far = []
    for index in range(rounds):
        far.append(from_partner(sending[..., index, :], "space", 1 << order[index]))
    far = jnp.stack(far, axis=-2)

    diff = far[:2] - own
    update = wc * diff
    adj_lat = far[2:] - g_own
    param_lat = face_weight * jnp.sum(g_f * diff, axis=2)

    kf = (0.5 * (cond[:-1] + cond[1:]))[:, None]
    kt = (0.5 * (therm[:-1] + therm[1:]))[:, None]
    d_p = p_old[1:] - p_old[:-1]
    d_t = t_old[1:] - t_old[:-1]
    flow = kf * d_p
    conduct = kt * d_t
    t_mean = 0.5 * (t_old[:-1] + t_old[1:])
    carried = flow * t_mean
    da = g_p[:-1] - g_p[1:]
    db = g_t[:-1] - g_t[1:]
    g_carried = 0.5 * db
    g_flow = da + g_carried * t_mean
    g_kf = jnp.sum(g_flow * d_p, axis=1)
    g_kt = jnp.sum(db * d_t, axis=1)
    vert_grads = jnp.stack([0.5 * pad_sum(g_kf, 0), 0.5 * pad_sum(g_kt, 0)])

    placed = exact_select(
        jnp.concatenate(
            [
                param_lat.reshape(2 * layers, rounds * face),
                jnp.concatenate([update, adj_lat]).reshape(4 * n_field, rounds * face),
            ]
        ),
        select,
        0,
    )
    lat_grads = placed[: 2 * layers].reshape(2, layers, width)
    lat = placed[2 * layers :].reshape(4, layers, members, width)
    grads = (vert_grads + lat_grads) * jnp.stack([cond, therm])
    owned = sum_scatter(grads, "member")


    p_rate = spread0(flow)
    p_rate = p_rate.at[0].add(recharge)
    t_rate = spread0(conduct) + 0.5 * spread0(carried)
    new_pressure = p_old + 0.1 * (p_rate + lat[0])
    new_heat = t_old + 0.1 * (t_rate + lat[1])
    adj_pressure = c_p - spread0(g_flow * kf) + lat[2]
    adj_heat = c_t - spread0(db * kt) + 0.5 * pad_sum(g_carried * flow, 0) + lat[3]
    outs = [new_pressure, new_heat, adj_pressure, adj_heat]
    return tuple(o.transpose(1, 0, 2) for o in outs) + (owned,)


def solution(mesh):
    placed = (
        P("member", None, "space"),
        P("member", None, "space"),
        P(None, "space"),
        P(None, "space"),
        P(None, "space"),
        P(None, "space"),
        P("member", "space"),
        P(None, "space"),
        P(None, "space"),
        P("member", None, "space"),
        P("member", None, "space"),
    )
    return jax.shard_map(
        body,
        mesh=mesh,
        in_specs=placed,
        out_specs=(
            P("member", None, "space"),
            P("member", None, "space"),
            P("member", None, "space"),
            P("member", None, "space"),
            P(None, None, ("space", "member")),
        ),
        check_vma=False,
    )
```

```python
import jax
import jax.numpy as jnp
from jax import lax
from jax.sharding import PartitionSpec as P


def from_partner(value, axis, mask):
    pairs = [(source, source ^ mask) for source in range(lax.axis_size(axis))]
    return lax.ppermute(value, axis, pairs)


def spread(grad_iface):
    return jnp.pad(grad_iface, ((0, 0), (0, 1), (0, 0))) - jnp.pad(
        grad_iface, ((0, 0), (1, 0), (0, 0))
    )


def spread0(grad_iface):
    return pad_sum(grad_iface, 0, -1.0)


def pad_sum(grad_iface, axis, sign=1.0):
    pads = [(0, 0)] * grad_iface.ndim
    low, high = list(pads), list(pads)
    low[axis], high[axis] = (0, 1), (1, 0)
    if sign < 0:
        return jnp.pad(grad_iface, low) - jnp.pad(grad_iface, high)
    return jnp.pad(grad_iface, low) + jnp.pad(grad_iface, high)


def split2(x):
    hi = lax.reduce_precision(x, exponent_bits=8, mantissa_bits=7)
    lo = x - hi
    return jnp.concatenate([hi.astype(jnp.bfloat16), lo.astype(jnp.bfloat16)])


def exact_select(rows, select, contract):
    n = rows.shape[0]
    parts = lax.dot_general(
        split2(rows),
        select,
        (((1,), (contract,)), ((), ())),
        preferred_element_type=jnp.float32,
    )
    return parts[:n] + parts[n:]


def reduce_scatter(value, axis):
    size = lax.axis_size(axis)
    index = lax.axis_index(axis)
    width = value.shape[-1] // size
    cur = value.reshape(value.shape[:-1] + (size, width))
    dist = size // 2
    while dist >= 1:
        half = cur.shape[-2] // 2
        lower, upper = cur[..., :half, :], cur[..., half:, :]
        bit = (index // dist) % 2 == 1
        keep = jnp.where(bit, upper, lower)
        send = jnp.where(bit, lower, upper)
        cur = keep + from_partner(send, axis, dist)
        dist //= 2
    return cur.reshape(value.shape[:-1] + (width,))


def sum_scatter(value, axis):
    size = lax.axis_size(axis)
    width = value.shape[-1] // size
    parts = jnp.moveaxis(value.reshape(value.shape[:-1] + (size, width)), -2, 0)
    got = lax.all_to_all(parts, axis, 0, 0, tiled=True)
    total = got[0]
    for index in range(1, size):
        total = total + got[index]
    return total


def body(
    pressure,
    heat,
    log_cond,
    log_therm,
    frozen,
    frozen_flag,
    recharge,
    face_cols,
    face_weight,
    cot_pressure,
    cot_heat,
):
    members, layers, width = pressure.shape
    rounds, face = face_cols.shape
    p_old = pressure.transpose(1, 0, 2)
    t_old = heat.transpose(1, 0, 2)
    c_p = cot_pressure.transpose(1, 0, 2)
    c_t = cot_heat.transpose(1, 0, 2)
    blocked = frozen * frozen_flag.astype(jnp.float32)
    cond = jnp.exp(log_cond - 3.0 * blocked)
    therm = jnp.exp(log_therm) * (1.0 + blocked)
    g_p = 0.1 * c_p
    g_t = 0.1 * c_t

    order = [3, 2, 0, 1] if rounds == 4 else list(range(rounds))
    face_cols = jnp.concatenate([face_cols[i : i + 1] for i in order])
    face_weight = jnp.concatenate([face_weight[i : i + 1] for i in order])
    cols = face_cols.reshape(rounds * face)
    select = (cols[:, None] == jnp.arange(width, dtype=jnp.int32)[None, :]).astype(
        jnp.bfloat16
    )

    n_field = members * layers
    rows = jnp.concatenate(
        [
            jnp.stack([p_old, t_old, c_p, c_t]).reshape(4 * n_field, width),
            jnp.stack([cond, therm]).reshape(2 * layers, width),
        ]
    )
    picked = exact_select(rows, select, 1)
    fields_f = picked[: 4 * n_field].reshape(4, layers, members, rounds, face)
    coefs_f = picked[4 * n_field :].reshape(2, layers, 1, rounds, face)
    wc = face_weight * coefs_f
    own = fields_f[:2]
    g_f = 0.1 * fields_f[2:]
    g_own = g_f * wc
    sending = jnp.concatenate([own, g_own])

    far = []
    for index in range(rounds):
        far.append(from_partner(sending[..., index, :], "space", 1 << order[index]))
    far = jnp.stack(far, axis=-2)

    diff = far[:2] - own
    update = wc * diff
    adj_lat = far[2:] - g_own
    param_lat = face_weight * jnp.sum(g_f * diff, axis=2)

    kf = (0.5 * (cond[:-1] + cond[1:]))[:, None]
    kt = (0.5 * (therm[:-1] + therm[1:]))[:, None]
    d_p = p_old[1:] - p_old[:-1]
    d_t = t_old[1:] - t_old[:-1]
    flow = kf * d_p
    conduct = kt * d_t
    t_mean = 0.5 * (t_old[:-1] + t_old[1:])
    carried = flow * t_mean
    da = g_p[:-1] - g_p[1:]
    db = g_t[:-1] - g_t[1:]
    g_carried = 0.5 * db
    g_flow = da + g_carried * t_mean
    g_kf = jnp.sum(g_flow * d_p, axis=1)
    g_kt = jnp.sum(db * d_t, axis=1)
    vert_grads = jnp.stack([0.5 * pad_sum(g_kf, 0), 0.5 * pad_sum(g_kt, 0)])

    placed = exact_select(
        jnp.concatenate(
            [
                param_lat.reshape(2 * layers, rounds * face),
                jnp.concatenate([update, adj_lat]).reshape(4 * n_field, rounds * face),
            ]
        ),
        select,
        0,
    )
    lat_grads = placed[: 2 * layers].reshape(2, layers, width)
    lat = placed[2 * layers :].reshape(4, layers, members, width)
    grads = (vert_grads + lat_grads) * jnp.stack([cond, therm])
    owned = sum_scatter(grads, "member")


    p_rate = spread0(flow)
    p_rate = p_rate.at[0].add(recharge)
    t_rate = spread0(conduct) + 0.5 * spread0(carried)
    new_pressure = p_old + 0.1 * (p_rate + lat[0])
    new_heat = t_old + 0.1 * (t_rate + lat[1])
    adj_pressure = c_p - spread0(g_flow * kf) + lat[2]
    adj_heat = c_t - spread0(db * kt) + 0.5 * pad_sum(g_carried * flow, 0) + lat[3]
    outs = [new_pressure, new_heat, adj_pressure, adj_heat]
    return tuple(o.transpose(1, 0, 2) for o in outs) + (owned,)


def solution(mesh):
    placed = (
        P("member", None, "space"),
        P("member", None, "space"),
        P(None, "space"),
        P(None, "space"),
        P(None, "space"),
        P(None, "space"),
        P("member", "space"),
        P(None, "space"),
        P(None, "space"),
        P("member", None, "space"),
        P("member", None, "space"),
    )
    return jax.shard_map(
        body,
        mesh=mesh,
        in_specs=placed,
        out_specs=(
            P("member", None, "space"),
            P("member", None, "space"),
            P("member", None, "space"),
            P("member", None, "space"),
            P(None, None, ("space", "member")),
        ),
        check_vma=False,
    )
```

```python
import jax
import jax.numpy as jnp
from jax import lax
from jax.sharding import PartitionSpec as P


def from_partner(value, axis, mask):
    pairs = [(source, source ^ mask) for source in range(lax.axis_size(axis))]
    return lax.ppermute(value, axis, pairs)


def spread(grad_iface):
    return jnp.pad(grad_iface, ((0, 0), (0, 1), (0, 0))) - jnp.pad(
        grad_iface, ((0, 0), (1, 0), (0, 0))
    )


def spread0(grad_iface):
    return pad_sum(grad_iface, 0, -1.0)


def pad_sum(grad_iface, axis, sign=1.0):
    pads = [(0, 0)] * grad_iface.ndim
    low, high = list(pads), list(pads)
    low[axis], high[axis] = (0, 1), (1, 0)
    if sign < 0:
        return jnp.pad(grad_iface, low) - jnp.pad(grad_iface, high)
    return jnp.pad(grad_iface, low) + jnp.pad(grad_iface, high)


def split2(x):
    hi = lax.reduce_precision(x, exponent_bits=8, mantissa_bits=7)
    lo = x - hi
    return jnp.concatenate([hi.astype(jnp.bfloat16), lo.astype(jnp.bfloat16)])


def exact_select(rows, select, contract):
    n = rows.shape[0]
    parts = lax.dot_general(
        split2(rows),
        select,
        (((1,), (contract,)), ((), ())),
        preferred_element_type=jnp.float32,
    )
    return parts[:n] + parts[n:]


def reduce_scatter(value, axis):
    size = lax.axis_size(axis)
    index = lax.axis_index(axis)
    width = value.shape[-1] // size
    cur = value.reshape(value.shape[:-1] + (size, width))
    dist = size // 2
    while dist >= 1:
        half = cur.shape[-2] // 2
        lower, upper = cur[..., :half, :], cur[..., half:, :]
        bit = (index // dist) % 2 == 1
        keep = jnp.where(bit, upper, lower)
        send = jnp.where(bit, lower, upper)
        cur = keep + from_partner(send, axis, dist)
        dist //= 2
    return cur.reshape(value.shape[:-1] + (width,))


def sum_scatter(value, axis):
    size = lax.axis_size(axis)
    width = value.shape[-1] // size
    parts = jnp.moveaxis(value.reshape(value.shape[:-1] + (size, width)), -2, 0)
    got = lax.all_to_all(parts, axis, 0, 0, tiled=True)
    total = got[0]
    for index in range(1, size):
        total = total + got[index]
    return total


def body(
    pressure,
    heat,
    log_cond,
    log_therm,
    frozen,
    frozen_flag,
    recharge,
    face_cols,
    face_weight,
    cot_pressure,
    cot_heat,
):
    members, layers, width = pressure.shape
    rounds, face = face_cols.shape
    p_old = pressure.transpose(1, 0, 2)
    t_old = heat.transpose(1, 0, 2)
    c_p = cot_pressure.transpose(1, 0, 2)
    c_t = cot_heat.transpose(1, 0, 2)
    blocked = frozen * frozen_flag.astype(jnp.float32)
    cond = jnp.exp(log_cond - 3.0 * blocked)
    therm = jnp.exp(log_therm) * (1.0 + blocked)
    g_p = 0.1 * c_p
    g_t = 0.1 * c_t

    order = [2, 0, 3, 1] if rounds == 4 else list(range(rounds))
    face_cols = jnp.concatenate([face_cols[i : i + 1] for i in order])
    face_weight = jnp.concatenate([face_weight[i : i + 1] for i in order])
    cols = face_cols.reshape(rounds * face)
    select = (cols[:, None] == jnp.arange(width, dtype=jnp.int32)[None, :]).astype(
        jnp.bfloat16
    )

    n_field = members * layers
    rows = jnp.concatenate(
        [
            jnp.stack([p_old, t_old, c_p, c_t]).reshape(4 * n_field, width),
            jnp.stack([cond, therm]).reshape(2 * layers, width),
        ]
    )
    picked = exact_select(rows, select, 1)
    fields_f = picked[: 4 * n_field].reshape(4, layers, members, rounds, face)
    coefs_f = picked[4 * n_field :].reshape(2, layers, 1, rounds, face)
    wc = face_weight * coefs_f
    own = fields_f[:2]
    g_f = 0.1 * fields_f[2:]
    g_own = g_f * wc
    sending = jnp.concatenate([own, g_own])

    far = []
    for index in range(rounds):
        far.append(from_partner(sending[..., index, :], "space", 1 << order[index]))
    far = jnp.stack(far, axis=-2)

    diff = far[:2] - own
    update = wc * diff
    adj_lat = far[2:] - g_own
    param_lat = face_weight * jnp.sum(g_f * diff, axis=2)

    kf = (0.5 * (cond[:-1] + cond[1:]))[:, None]
    kt = (0.5 * (therm[:-1] + therm[1:]))[:, None]
    d_p = p_old[1:] - p_old[:-1]
    d_t = t_old[1:] - t_old[:-1]
    flow = kf * d_p
    conduct = kt * d_t
    t_mean = 0.5 * (t_old[:-1] + t_old[1:])
    carried = flow * t_mean
    da = g_p[:-1] - g_p[1:]
    db = g_t[:-1] - g_t[1:]
    g_carried = 0.5 * db
    g_flow = da + g_carried * t_mean
    g_kf = jnp.sum(g_flow * d_p, axis=1)
    g_kt = jnp.sum(db * d_t, axis=1)
    vert_grads = jnp.stack([0.5 * pad_sum(g_kf, 0), 0.5 * pad_sum(g_kt, 0)])

    placed = exact_select(
        jnp.concatenate(
            [
                param_lat.reshape(2 * layers, rounds * face),
                jnp.concatenate([update, adj_lat]).reshape(4 * n_field, rounds * face),
            ]
        ),
        select,
        0,
    )
    lat_grads = placed[: 2 * layers].reshape(2, layers, width)
    lat = placed[2 * layers :].reshape(4, layers, members, width)
    grads = (vert_grads + lat_grads) * jnp.stack([cond, therm])
    owned = sum_scatter(grads, "member")


    p_rate = spread0(flow)
    p_rate = p_rate.at[0].add(recharge)
    t_rate = spread0(conduct) + 0.5 * spread0(carried)
    new_pressure = p_old + 0.1 * (p_rate + lat[0])
    new_heat = t_old + 0.1 * (t_rate + lat[1])
    adj_pressure = c_p - spread0(g_flow * kf) + lat[2]
    adj_heat = c_t - spread0(db * kt) + 0.5 * pad_sum(g_carried * flow, 0) + lat[3]
    outs = [new_pressure, new_heat, adj_pressure, adj_heat]
    return tuple(o.transpose(1, 0, 2) for o in outs) + (owned,)


def solution(mesh):
    placed = (
        P("member", None, "space"),
        P("member", None, "space"),
        P(None, "space"),
        P(None, "space"),
        P(None, "space"),
        P(None, "space"),
        P("member", "space"),
        P(None, "space"),
        P(None, "space"),
        P("member", None, "space"),
        P("member", None, "space"),
    )
    return jax.shard_map(
        body,
        mesh=mesh,
        in_specs=placed,
        out_specs=(
            P("member", None, "space"),
            P("member", None, "space"),
            P("member", None, "space"),
            P("member", None, "space"),
            P(None, None, ("space", "member")),
        ),
        check_vma=False,
    )
```

```python
import jax
import jax.numpy as jnp
from jax import lax
from jax.sharding import PartitionSpec as P


def from_partner(value, axis, mask):
    pairs = [(source, source ^ mask) for source in range(lax.axis_size(axis))]
    return lax.ppermute(value, axis, pairs)


def spread(grad_iface):
    return jnp.pad(grad_iface, ((0, 0), (0, 1), (0, 0))) - jnp.pad(
        grad_iface, ((0, 0), (1, 0), (0, 0))
    )


def spread0(grad_iface):
    return pad_sum(grad_iface, 0, -1.0)


def pad_sum(grad_iface, axis, sign=1.0):
    pads = [(0, 0)] * grad_iface.ndim
    low, high = list(pads), list(pads)
    low[axis], high[axis] = (0, 1), (1, 0)
    if sign < 0:
        return jnp.pad(grad_iface, low) - jnp.pad(grad_iface, high)
    return jnp.pad(grad_iface, low) + jnp.pad(grad_iface, high)


def split2(x):
    hi = lax.reduce_precision(x, exponent_bits=8, mantissa_bits=7)
    lo = x - hi
    return jnp.concatenate([hi.astype(jnp.bfloat16), lo.astype(jnp.bfloat16)])


def exact_select(rows, select, contract):
    n = rows.shape[0]
    parts = lax.dot_general(
        split2(rows),
        select,
        (((1,), (contract,)), ((), ())),
        preferred_element_type=jnp.float32,
    )
    return parts[:n] + parts[n:]


def reduce_scatter(value, axis):
    size = lax.axis_size(axis)
    index = lax.axis_index(axis)
    width = value.shape[-1] // size
    cur = value.reshape(value.shape[:-1] + (size, width))
    dist = size // 2
    while dist >= 1:
        half = cur.shape[-2] // 2
        lower, upper = cur[..., :half, :], cur[..., half:, :]
        bit = (index // dist) % 2 == 1
        keep = jnp.where(bit, upper, lower)
        send = jnp.where(bit, lower, upper)
        cur = keep + from_partner(send, axis, dist)
        dist //= 2
    return cur.reshape(value.shape[:-1] + (width,))


def sum_scatter(value, axis):
    size = lax.axis_size(axis)
    width = value.shape[-1] // size
    parts = jnp.moveaxis(value.reshape(value.shape[:-1] + (size, width)), -2, 0)
    got = lax.all_to_all(parts, axis, 0, 0, tiled=True)
    total = got[0]
    for index in range(1, size):
        total = total + got[index]
    return total


def body(
    pressure,
    heat,
    log_cond,
    log_therm,
    frozen,
    frozen_flag,
    recharge,
    face_cols,
    face_weight,
    cot_pressure,
    cot_heat,
):
    members, layers, width = pressure.shape
    rounds, face = face_cols.shape
    p_old = pressure.transpose(1, 0, 2)
    t_old = heat.transpose(1, 0, 2)
    c_p = cot_pressure.transpose(1, 0, 2)
    c_t = cot_heat.transpose(1, 0, 2)
    blocked = frozen * frozen_flag.astype(jnp.float32)
    cond = jnp.exp(log_cond - 3.0 * blocked)
    therm = jnp.exp(log_therm) * (1.0 + blocked)
    g_p = 0.1 * c_p
    g_t = 0.1 * c_t

    order = [2, 3, 0, 1] if rounds == 4 else list(range(rounds))
    face_cols = jnp.concatenate([face_cols[i : i + 1] for i in order])
    face_weight = jnp.concatenate([face_weight[i : i + 1] for i in order])
    cols = face_cols.reshape(rounds * face)
    select = (cols[:, None] == jnp.arange(width, dtype=jnp.int32)[None, :]).astype(
        jnp.bfloat16
    )

    n_field = members * layers
    rows = jnp.concatenate(
        [
            jnp.stack([p_old, t_old, c_p, c_t]).reshape(4 * n_field, width),
            jnp.stack([cond, therm]).reshape(2 * layers, width),
        ]
    )
    picked = exact_select(rows, select, 1)
    fields_f = picked[: 4 * n_field].reshape(4, layers, members, rounds, face)
    coefs_f = picked[4 * n_field :].reshape(2, layers, 1, rounds, face)
    wc = face_weight * coefs_f
    own = fields_f[:2]
    g_f = 0.1 * fields_f[2:]
    g_own = g_f * wc
    sending = jnp.concatenate([own, g_own])

    far = []
    for index in range(rounds):
        far.append(from_partner(sending[..., index, :], "space", 1 << order[index]))
    far = jnp.stack(far, axis=-2)

    diff = far[:2] - own
    update = wc * diff
    adj_lat = far[2:] - g_own
    param_lat = face_weight * jnp.sum(g_f * diff, axis=2)

    kf = (0.5 * (cond[:-1] + cond[1:]))[:, None]
    kt = (0.5 * (therm[:-1] + therm[1:]))[:, None]
    d_p = p_old[1:] - p_old[:-1]
    d_t = t_old[1:] - t_old[:-1]
    flow = kf * d_p
    conduct = kt * d_t
    t_mean = 0.5 * (t_old[:-1] + t_old[1:])
    carried = flow * t_mean
    da = g_p[:-1] - g_p[1:]
    db = g_t[:-1] - g_t[1:]
    g_carried = 0.5 * db
    g_flow = da + g_carried * t_mean
    g_kf = jnp.sum(g_flow * d_p, axis=1)
    g_kt = jnp.sum(db * d_t, axis=1)
    vert_grads = jnp.stack([0.5 * pad_sum(g_kf, 0), 0.5 * pad_sum(g_kt, 0)])

    lat_grads = exact_select(
        param_lat.reshape(2 * layers, rounds * face), select, 0
    ).reshape(2, layers, width)
    grads = (vert_grads + lat_grads) * jnp.stack([cond, therm])
    owned = sum_scatter(grads, "member")
    lat = exact_select(
        jnp.concatenate([update, adj_lat]).reshape(4 * n_field, rounds * face),
        select,
        0,
    ).reshape(4, layers, members, width)


    p_rate = spread0(flow)
    p_rate = p_rate.at[0].add(recharge)
    t_rate = spread0(conduct) + 0.5 * spread0(carried)
    new_pressure = p_old + 0.1 * (p_rate + lat[0])
    new_heat = t_old + 0.1 * (t_rate + lat[1])
    adj_pressure = c_p - spread0(g_flow * kf) + lat[2]
    adj_heat = c_t - spread0(db * kt) + 0.5 * pad_sum(g_carried * flow, 0) + lat[3]
    outs = [new_pressure, new_heat, adj_pressure, adj_heat]
    return tuple(o.transpose(1, 0, 2) for o in outs) + (owned,)


def solution(mesh):
    placed = (
        P("member", None, "space"),
        P("member", None, "space"),
        P(None, "space"),
        P(None, "space"),
        P(None, "space"),
        P(None, "space"),
        P("member", "space"),
        P(None, "space"),
        P(None, "space"),
        P("member", None, "space"),
        P("member", None, "space"),
    )
    return jax.shard_map(
        body,
        mesh=mesh,
        in_specs=placed,
        out_specs=(
            P("member", None, "space"),
            P("member", None, "space"),
            P("member", None, "space"),
            P("member", None, "space"),
            P(None, None, ("space", "member")),
        ),
        check_vma=False,
    )
```

```python
import jax
import jax.numpy as jnp
from jax import lax
from jax.sharding import PartitionSpec as P


def from_partner(value, axis, mask):
    pairs = [(source, source ^ mask) for source in range(lax.axis_size(axis))]
    return lax.ppermute(value, axis, pairs)


def spread(grad_iface):
    return jnp.pad(grad_iface, ((0, 0), (0, 1), (0, 0))) - jnp.pad(
        grad_iface, ((0, 0), (1, 0), (0, 0))
    )


def spread0(grad_iface):
    return pad_sum(grad_iface, 0, -1.0)


def pad_sum(grad_iface, axis, sign=1.0):
    pads = [(0, 0)] * grad_iface.ndim
    low, high = list(pads), list(pads)
    low[axis], high[axis] = (0, 1), (1, 0)
    if sign < 0:
        return jnp.pad(grad_iface, low) - jnp.pad(grad_iface, high)
    return jnp.pad(grad_iface, low) + jnp.pad(grad_iface, high)


def split2(x):
    hi = lax.reduce_precision(x, exponent_bits=8, mantissa_bits=7)
    lo = x - hi
    return jnp.concatenate([hi.astype(jnp.bfloat16), lo.astype(jnp.bfloat16)])


def exact_select(rows, select, contract):
    n = rows.shape[0]
    parts = lax.dot_general(
        split2(rows),
        select,
        (((1,), (contract,)), ((), ())),
        preferred_element_type=jnp.float32,
    )
    return parts[:n] + parts[n:]


def reduce_scatter(value, axis):
    size = lax.axis_size(axis)
    index = lax.axis_index(axis)
    width = value.shape[-1] // size
    cur = value.reshape(value.shape[:-1] + (size, width))
    dist = size // 2
    while dist >= 1:
        half = cur.shape[-2] // 2
        lower, upper = cur[..., :half, :], cur[..., half:, :]
        bit = (index // dist) % 2 == 1
        keep = jnp.where(bit, upper, lower)
        send = jnp.where(bit, lower, upper)
        cur = keep + from_partner(send, axis, dist)
        dist //= 2
    return cur.reshape(value.shape[:-1] + (width,))


def sum_scatter(value, axis):
    size = lax.axis_size(axis)
    width = value.shape[-1] // size
    parts = jnp.moveaxis(value.reshape(value.shape[:-1] + (size, width)), -2, 0)
    got = lax.all_to_all(parts, axis, 0, 0, tiled=True)
    total = got[0]
    for index in range(1, size):
        total = total + got[index]
    return total


def body(
    pressure,
    heat,
    log_cond,
    log_therm,
    frozen,
    frozen_flag,
    recharge,
    face_cols,
    face_weight,
    cot_pressure,
    cot_heat,
):
    members, layers, width = pressure.shape
    rounds, face = face_cols.shape
    p_old = pressure.transpose(1, 0, 2)
    t_old = heat.transpose(1, 0, 2)
    c_p = cot_pressure.transpose(1, 0, 2)
    c_t = cot_heat.transpose(1, 0, 2)
    blocked = frozen * frozen_flag.astype(jnp.float32)
    cond = jnp.exp(log_cond - 3.0 * blocked)
    therm = jnp.exp(log_therm) * (1.0 + blocked)
    g_p = 0.1 * c_p
    g_t = 0.1 * c_t

    order = [2, 3, 0, 1] if rounds == 4 else list(range(rounds))
    face_cols = jnp.concatenate([face_cols[i : i + 1] for i in order])
    face_weight = jnp.concatenate([face_weight[i : i + 1] for i in order])
    cols = face_cols.reshape(rounds * face)
    select = (cols[:, None] == jnp.arange(width, dtype=jnp.int32)[None, :]).astype(
        jnp.bfloat16
    )

    n_field = members * layers
    rows = jnp.concatenate(
        [
            jnp.stack([p_old, t_old, c_p, c_t]).reshape(4 * n_field, width),
            jnp.stack([cond, therm]).reshape(2 * layers, width),
        ]
    )
    picked = exact_select(rows, select, 1)
    fields_f = picked[: 4 * n_field].reshape(4, layers, members, rounds, face)
    coefs_f = picked[4 * n_field :].reshape(2, layers, 1, rounds, face)
    wc = face_weight * coefs_f
    own = fields_f[:2]
    g_f = 0.1 * fields_f[2:]
    g_own = g_f * wc
    sending = jnp.concatenate([own, g_own])

    far = []
    for index in range(rounds):
        far.append(from_partner(sending[..., index, :], "space", 1 << order[index]))
    far = jnp.stack(far, axis=-2)

    diff = far[:2] - own
    update = wc * diff
    adj_lat = far[2:] - g_own
    param_lat = face_weight * jnp.sum(g_f * diff, axis=2)

    kf = (0.5 * (cond[:-1] + cond[1:]))[:, None]
    kt = (0.5 * (therm[:-1] + therm[1:]))[:, None]
    d_p = p_old[1:] - p_old[:-1]
    d_t = t_old[1:] - t_old[:-1]
    flow = kf * d_p
    conduct = kt * d_t
    t_mean = 0.5 * (t_old[:-1] + t_old[1:])
    carried = flow * t_mean
    da = g_p[:-1] - g_p[1:]
    db = g_t[:-1] - g_t[1:]
    g_carried = 0.5 * db
    g_flow = da + g_carried * t_mean
    g_kf = jnp.sum(g_flow * d_p, axis=1)
    g_kt = jnp.sum(db * d_t, axis=1)
    vert_grads = jnp.stack([0.5 * pad_sum(g_kf, 0), 0.5 * pad_sum(g_kt, 0)])

    lat_grads = exact_select(
        param_lat.reshape(2 * layers, rounds * face), select, 0
    ).reshape(2, layers, width)
    grads = (vert_grads + lat_grads) * jnp.stack([cond, therm])
    owned = sum_scatter(grads, "member")
    lat_parts = lax.dot_general(
        split2(jnp.concatenate([update, adj_lat]).reshape(4 * n_field, rounds * face)),
        select,
        (((1,), (0,)), ((), ())),
        preferred_element_type=jnp.float32,
    ).reshape(2, 4, layers, members, width)
    lat = [lat_parts[0, i] + lat_parts[1, i] for i in range(4)]


    p_rate = spread0(flow)
    p_rate = p_rate.at[0].add(recharge)
    t_rate = spread0(conduct) + 0.5 * spread0(carried)
    new_pressure = p_old + 0.1 * (p_rate + lat[0])
    new_heat = t_old + 0.1 * (t_rate + lat[1])
    adj_pressure = c_p - spread0(g_flow * kf) + lat[2]
    adj_heat = c_t - spread0(db * kt) + 0.5 * pad_sum(g_carried * flow, 0) + lat[3]
    outs = [new_pressure, new_heat, adj_pressure, adj_heat]
    return tuple(o.transpose(1, 0, 2) for o in outs) + (owned,)


def solution(mesh):
    placed = (
        P("member", None, "space"),
        P("member", None, "space"),
        P(None, "space"),
        P(None, "space"),
        P(None, "space"),
        P(None, "space"),
        P("member", "space"),
        P(None, "space"),
        P(None, "space"),
        P("member", None, "space"),
        P("member", None, "space"),
    )
    return jax.shard_map(
        body,
        mesh=mesh,
        in_specs=placed,
        out_specs=(
            P("member", None, "space"),
            P("member", None, "space"),
            P("member", None, "space"),
            P("member", None, "space"),
            P(None, None, ("space", "member")),
        ),
        check_vma=False,
    )
```
